32 devices in a mesh: dom: 8 (over y, x, core), sub: 4 (over z).
Axes of the slice: x: 2, y: 2, z: 4, core: 2. Of those that a mesh axis runs over, the one named last changes fastest.
Arguments:
- vectors: bfloat16 [8192, 1024], P(('dom', 'sub')), may hold values from -8 to 8
- assign: int32 [8192], P(('dom', 'sub')), may hold values from 0 to 32767, as said below
- codes: int32 [8192, 256], P(('dom', 'sub')), may hold values from 0 to 15
- centroids: float32 [32768, 1024], P('dom', 'sub'), may hold values from -4 to 4
- perp_ratio: float32 [32768], P('dom'), may hold values from 0.25 to 0.9
- codebook: float32 [256, 16, 4], P('sub'), may hold values from -4 to 4
- codeword_weight_total: float32 [256, 16], P('sub'), may hold values from 64 to 512
Outputs:
- new_centroids: float32 [32768, 1024], P('dom', 'sub')
- residual: bfloat16 [8192, 1024], P(('dom', 'sub'))
- new_codebook: float32 [256, 16, 4], P('sub')
The draws below stay inside these ranges and needn't reach their ends.
Inputs may be any that keep to these rules, and one draw needn't show every extreme that they name: `assign`: owner o holds partitions o * 4096 to (o + 1) * 4096 - 1 and o runs over 8 owners. The rows of one device are grouped by owner in increasing owner order; at most 64 rows of one device belong to one owner, and on every device some owner receives exactly 64.
All inputs are finite; a program needn't handle non-finite values.
Results may differ from the reference program's by a relative error of at most 0.001.
Values may be sent and summed in bfloat16 or wider, within the bound.
No kernel may reach another device: no remote copies, remote signals or barrier semaphores. Data moves between devices by JAX's collectives and lax.ppermute only.
A program may use at most 128 MiB of HBM per device.

```python
import math
import jax
import jax.numpy as jnp

D = 1024
PARTS_SIZE = 32768
K = 16
DS = 4
ITERS = 4
R_DEV = 256
OWNERS = 8
ROW_HOLDERS = 32
ROWS = 8192
CAP = 64
PART_DEV = 4096
M = 256


def owner_table(key):
    base_key = jax.random.fold_in(key, 11)
    remaining_peers = OWNERS - 1
    spare = R_DEV - CAP
    levels = spare // remaining_peers
    remainder_rows = spare - levels * remaining_peers
    pair_count = remaining_peers // 2
    shuffle = jax.random.permutation(jax.random.fold_in(base_key, 2), OWNERS)
    hot_pool = max(1, OWNERS // 4)
    hot_pick = jax.random.randint(jax.random.fold_in(base_key, 3), (ROW_HOLDERS,), 0, hot_pool)
    hot_owner = shuffle[hot_pick]
    jitter = jax.random.randint(jax.random.fold_in(base_key, 4), (ROW_HOLDERS, pair_count), -(levels // 2), levels // 2 + 1)
    row_distribution = jnp.full((ROW_HOLDERS, remaining_peers), levels, jnp.int32)
    row_distribution = row_distribution.at[:, 0:2 * pair_count:2].add(jitter)
    row_distribution = row_distribution.at[:, 1:2 * pair_count:2].add(-jitter)
    extra_rows = (jnp.arange(remaining_peers) < remainder_rows).astype(jnp.int32)
    row_distribution = row_distribution + extra_rows[None, :]
    values = jnp.concatenate([jnp.full((ROW_HOLDERS, 1), CAP, jnp.int32), row_distribution], axis=1)
    place_keys = jax.random.split(jax.random.fold_in(base_key, 1), ROW_HOLDERS)

    def place(one_key, hot_one, row_values):
        order = jax.random.permutation(one_key, OWNERS)
        where_hot = jnp.argmax(order == hot_one)
        leading = order[0]
        order = order.at[where_hot].set(leading).at[0].set(hot_one)
        return jnp.zeros((OWNERS,), jnp.int32).at[order].set(row_values)
    return jax.vmap(place)(place_keys, hot_owner, values)


def code_table(key):
    return jax.random.randint(jax.random.fold_in(key, 31), (ROWS, M), 0, K)


def draw_assign(key, part):
    counts = owner_table(key)
    ends = jnp.cumsum(counts, axis=1)
    position = jnp.arange(R_DEV, dtype=jnp.int32)
    owner_of = jnp.sum((ends[:, None, :] <= position[None, :, None]).astype(jnp.int32), axis=2)
    within = jax.random.randint(jax.random.fold_in(key, 21), (ROW_HOLDERS, R_DEV), 0, PART_DEV)
    return (owner_of * PART_DEV + within).reshape(ROW_HOLDERS * R_DEV).astype(jnp.int32)


def draw_codes(key, part):
    return code_table(key)


def draw_vectors(key, part):
    code_ids = code_table(key)
    noise = jax.random.truncated_normal(jax.random.fold_in(key, 41), -4.0, 4.0, (ROWS, D), jnp.float32)
    table = jax.random.truncated_normal(jax.random.fold_in(key, 42), -3.0, 3.0, (M * K, DS), jnp.float32)
    lookup = jnp.arange(M, dtype=jnp.int32)[None, :] * K + code_ids
    offsets = table[lookup].reshape(ROWS, D)
    return (noise + offsets).astype(jnp.bfloat16)


def shard_levels(key, shape, shards, smallest, top_value):
    factor_of = 1.0
    for dim, parts in shards:
        draws = jax.random.uniform(jax.random.fold_in(jax.random.fold_in(key, 6), dim), (parts,), jnp.float32, smallest / len(shards), top_value / len(shards))
        factor_of = factor_of * jnp.repeat(jnp.exp(draws), shape[dim] // parts).reshape((-1,) + (1,) * (len(shape) - 1 - dim))
    return factor_of


def centred(own_key, extent, scale, bound, shards=(), held_as=jnp.bfloat16):
    drawn = scale * jax.random.normal(own_key, extent, jnp.float32)
    if shards:
        drawn = drawn * shard_levels(own_key, extent, shards, -0.22, 0.18)
    return jnp.clip(drawn, -bound, bound).astype(held_as)


def setup_inputs(seed: int = 0) -> dict:
    arg_keys = jax.random.split(jax.random.key(seed), 8)
    return {
        "vectors": draw_vectors(jax.random.fold_in(arg_keys[7], 71), 0),
        "assign": draw_assign(jax.random.fold_in(arg_keys[7], 71), 0),
        "codes": draw_codes(jax.random.fold_in(arg_keys[7], 71), 0),
        "centroids": centred(arg_keys[3], (PARTS_SIZE, D), 1.0, 4.0, ((0, 8), (1, 4)), jnp.float32),
        "perp_ratio": jnp.clip(jnp.exp(math.log(0.9) - 1.2809338 * jax.random.uniform(arg_keys[4], (PARTS_SIZE,), jnp.float32) ** shard_levels(arg_keys[4], (PARTS_SIZE,), ((0, 8),), -0.2, 0.2)), 0.25, 0.9),
        "codebook": centred(arg_keys[5], (M, K, DS), 1.0, 4.0, ((0, 4),), jnp.float32),
        "codeword_weight_total": jnp.clip(jnp.exp(math.log(512.0) - 2.0794415 * jax.random.uniform(arg_keys[6], (M, K), jnp.float32) ** shard_levels(arg_keys[6], (M, K), ((0, 4),), -0.2, 0.2)), 64.0, 512.0),
    }


def reference(vectors, assign, codes, centroids, perp_ratio, codebook, codeword_weight_total):
    rows = vectors.astype(jnp.float32)
    unit_mass = jnp.ones((rows.shape[0],), jnp.float32)
    filled = jax.ops.segment_sum(unit_mass, assign, num_segments=PARTS_SIZE)
    sum_x = jax.ops.segment_sum(rows, assign, num_segments=PARTS_SIZE)
    norms = jnp.sum(rows * rows, axis=1)
    floors = jnp.maximum(filled, 1.0)[:, None]
    weight_fractions = perp_ratio[:, None]
    current = centroids
    for iteration in range(ITERS):
        picked = jnp.take(current, assign, axis=0)
        weight = jnp.sum(rows * picked, axis=1) / (norms + 1e-6)
        projected = jax.ops.segment_sum(rows * weight[:, None], assign, num_segments=PARTS_SIZE)
        current = current - (weight_fractions * filled[:, None] * current + (1.0 - weight_fractions) * projected - sum_x) / floors
    residual = (rows - jnp.take(current, assign, axis=0)).astype(jnp.bfloat16)
    pieces = residual.astype(jnp.float32).reshape(-1, DS)
    code_keys = (jnp.arange(M, dtype=jnp.int32)[None, :] * K + codes).reshape(-1)
    book_sums = jax.ops.segment_sum(pieces, code_keys, num_segments=M * K)
    book_counts = jax.ops.segment_sum(jnp.ones(code_keys.shape, jnp.float32), code_keys, num_segments=M * K)
    weights = codeword_weight_total.reshape(M * K, 1)
    updated = (codebook.reshape(M * K, DS) * weights + book_sums) / (weights + book_counts[:, None])
    return current, residual, updated.reshape(M, K, DS)
```

```python
import jax
import jax.numpy as jnp
from jax import lax
from jax.sharding import PartitionSpec as P

ITERS = 4
ID_BASE = 64


def split_dot(table, values):
    high = lax.reduce_precision(values, exponent_bits=8, mantissa_bits=7)
    low = (values - high).astype(jnp.bfloat16)
    width = values.shape[1]
    parts = jnp.concatenate([high.astype(jnp.bfloat16), low], axis=1)
    both = jnp.dot(table, parts, preferred_element_type=jnp.float32)
    return both[:, :width] + both[:, width:]


def per_device(vectors, assign, codes, centroids, perp_ratio, codebook, codeword_weight_total):
    owners = lax.axis_size("dom")
    sub_count = lax.axis_size("sub")
    rows_dev, row_width = vectors.shape
    part_local, columns = centroids.shape
    local_sub, code_count, sub_dim = codebook.shape
    capacity = 2 * rows_dev // owners

    owner_of = assign // part_local
    owner_mask = owner_of[:, None] == jnp.arange(owners, dtype=jnp.int32)[None, :]
    counts = jnp.sum(owner_mask.astype(jnp.int32), axis=0)
    starts = jnp.cumsum(counts) - counts
    first_row_index = jnp.sum(jnp.where(owner_mask, starts[None, :], 0), axis=1)
    position = jnp.arange(rows_dev, dtype=jnp.int32) - first_row_index
    slot_index = owner_of * capacity + position
    source_rows = starts[:, None] + jnp.arange(capacity, dtype=jnp.int32)[None, :]
    usable_slot = jnp.arange(capacity, dtype=jnp.int32)[None, :] < counts[:, None]
    clipped = jnp.minimum(source_rows, rows_dev - 1)
    send_rows = jnp.where(
        usable_slot[:, :, None], jnp.take(vectors, clipped, axis=0), jnp.zeros((), jnp.bfloat16)
    )
    send_codes = jnp.take(codes, clipped, axis=0).astype(jnp.bfloat16)
    owner_base = (jnp.arange(owners, dtype=jnp.int32) * part_local)[:, None]
    send_ids = jnp.where(usable_slot, jnp.take(assign, clipped, axis=0) - owner_base, part_local)
    id_parts = jnp.stack([send_ids // ID_BASE, send_ids % ID_BASE], axis=-1).astype(jnp.bfloat16)
    packet = jnp.concatenate(
        [
            send_rows.reshape(owners, capacity, sub_count, columns),
            send_codes.reshape(owners, capacity, sub_count, local_sub),
            jnp.broadcast_to(id_parts[:, :, None, :], (owners, capacity, sub_count, 2)),
        ],
        axis=-1,
    )
    width = packet.shape[-1]
    packet = packet.transpose(0, 2, 1, 3).reshape(owners * sub_count, capacity, width)
    arrived = lax.all_to_all(packet, ("dom", "sub"), split_axis=0, concat_axis=0, tiled=True)
    arrived = arrived.reshape(-1, width)

    rows = arrived[:, :columns]
    row_codes = arrived[:, columns : columns + local_sub].astype(jnp.int32)
    id_floats = arrived[:, columns + local_sub :].astype(jnp.float32)
    slot_ids = (id_floats[:, 0] * ID_BASE + id_floats[:, 1]).astype(jnp.int32)
    usable = slot_ids < part_local
    safe_ids = jnp.minimum(slot_ids, part_local - 1)

    same = (slot_ids[:, None] == slot_ids[None, :]) & usable[:, None]
    same_table = same.astype(jnp.bfloat16)
    filled = jnp.sum(same.astype(jnp.float32), axis=1)
    floors = jnp.maximum(filled, 1.0)[:, None]
    sum_x = jnp.dot(same_table, rows, preferred_element_type=jnp.float32)
    as_float = rows.astype(jnp.float32)
    current = jnp.take(centroids, safe_ids, axis=0)
    weight_fractions = jnp.take(perp_ratio, safe_ids)[:, None]
    filled_fraction = weight_fractions * filled[:, None]
    stats = lax.psum(
        jnp.stack([jnp.sum(as_float * as_float, axis=1), jnp.sum(as_float * current, axis=1)]), "sub"
    )
    norms = stats[0]
    inner = stats[1]
    for iteration in range(ITERS):
        if iteration > 0:
            inner = lax.psum(jnp.sum(as_float * current, axis=1), "sub")
        weight = inner / (norms + 1e-06)
        projected = split_dot(same_table, as_float * weight[:, None])
        current = (
            current
            - (filled_fraction * current + (1.0 - weight_fractions) * projected - sum_x) / floors
        )
    write_ids = jnp.where(usable, slot_ids, part_local)
    new_centroids = centroids.at[write_ids].set(current, mode="drop")
    residual = jnp.where(usable[:, None], as_float - current, 0.0).astype(jnp.bfloat16)

    code_member = (
        (row_codes[:, :, None] == jnp.arange(code_count, dtype=jnp.int32)[None, None, :])
        & usable[:, None, None]
    ).astype(jnp.bfloat16)
    pieces = residual.reshape(-1, local_sub, sub_dim)
    book_sums = jnp.einsum("rmk,rmd->mkd", code_member, pieces, preferred_element_type=jnp.float32)
    book_counts = jnp.sum(code_member, axis=0, dtype=jnp.float32)
    packed = jnp.concatenate([book_sums.reshape(-1), book_counts.reshape(-1)])
    packed = lax.psum(packed.reshape(-1, 128), "dom").reshape(-1)
    entries = local_sub * code_count
    totals = packed[: entries * sub_dim].reshape(entries, sub_dim)
    tallies = packed[entries * sub_dim :]
    weights = codeword_weight_total.reshape(entries, 1)
    updated = (codebook.reshape(entries, sub_dim) * weights + totals) / (weights + tallies[:, None])

    outgoing = residual.reshape(owners * sub_count, capacity, columns)
    returned = lax.all_to_all(outgoing, ("dom", "sub"), split_axis=0, concat_axis=0, tiled=True)
    returned = returned.reshape(owners, sub_count, capacity, columns).transpose(0, 2, 1, 3)
    flat_rows = returned.reshape(owners * capacity, row_width)
    residual_rows = jnp.take(flat_rows, slot_index, axis=0)
    return (new_centroids, residual_rows, updated.reshape(local_sub, code_count, sub_dim))


def solution(mesh):
    placed = (
        P(("dom", "sub"), None),
        P(("dom", "sub")),
        P(("dom", "sub"), None),
        P("dom", "sub"),
        P("dom"),
        P("sub", None, None),
        P("sub", None),
    )
    return jax.shard_map(
        per_device,
        mesh=mesh,
        in_specs=placed,
        out_specs=(P("dom", "sub"), P(("dom", "sub"), None), P("sub", None, None)),
        check_vma=False,
    )
```

```python
import jax
import jax.numpy as jnp
from jax import lax
from jax.sharding import PartitionSpec as P

ITERS = 4
ID_BASE = 64


def split_dot(table, values):
    high = lax.reduce_precision(values, exponent_bits=8, mantissa_bits=7)
    low = (values - high).astype(jnp.bfloat16)
    width = values.shape[1]
    parts = jnp.concatenate([high.astype(jnp.bfloat16), low], axis=1)
    both = jnp.dot(table, parts, preferred_element_type=jnp.float32)
    return both[:, :width] + both[:, width:]


def exact_pick(pick, values):
    high = lax.reduce_precision(values, exponent_bits=8, mantissa_bits=7)
    rest = values - high
    middle = lax.reduce_precision(rest, exponent_bits=8, mantissa_bits=7)
    low = rest - middle
    parts = jnp.stack([high, middle, low], axis=1).astype(jnp.bfloat16)
    picked = jnp.dot(pick, parts, preferred_element_type=jnp.float32)
    return (picked[:, 0] + picked[:, 1]) + picked[:, 2]


def per_device(vectors, assign, codes, centroids, perp_ratio, codebook, codeword_weight_total):
    owners = lax.axis_size("dom")
    sub_count = lax.axis_size("sub")
    rows_dev, row_width = vectors.shape
    part_local, columns = centroids.shape
    local_sub, code_count, sub_dim = codebook.shape
    capacity = 2 * rows_dev // owners

    owner_of = assign // part_local
    owner_mask = owner_of[:, None] == jnp.arange(owners, dtype=jnp.int32)[None, :]
    counts = jnp.sum(owner_mask.astype(jnp.int32), axis=0)
    starts = jnp.cumsum(counts) - counts
    first_row_index = jnp.sum(jnp.where(owner_mask, starts[None, :], 0), axis=1)
    position = jnp.arange(rows_dev, dtype=jnp.int32) - first_row_index
    slot_index = owner_of * capacity + position
    source_rows = starts[:, None] + jnp.arange(capacity, dtype=jnp.int32)[None, :]
    usable_slot = jnp.arange(capacity, dtype=jnp.int32)[None, :] < counts[:, None]
    clipped = jnp.minimum(source_rows, rows_dev - 1)
    send_rows = jnp.where(
        usable_slot[:, :, None], jnp.take(vectors, clipped, axis=0), jnp.zeros((), jnp.bfloat16)
    )
    send_codes = jnp.take(codes, clipped, axis=0).astype(jnp.bfloat16)
    owner_base = (jnp.arange(owners, dtype=jnp.int32) * part_local)[:, None]
    send_ids = jnp.where(usable_slot, jnp.take(assign, clipped, axis=0) - owner_base, part_local)
    id_parts = jnp.stack([send_ids // ID_BASE, send_ids % ID_BASE], axis=-1).astype(jnp.bfloat16)
    split_rows = send_rows.reshape(owners, capacity, sub_count, columns).transpose(0, 2, 1, 3)
    split_rows = split_rows.reshape(owners * sub_count, capacity, columns)
    meta = jnp.concatenate(
        [
            send_codes.reshape(owners, capacity, sub_count, local_sub),
            jnp.broadcast_to(id_parts[:, :, None, :], (owners, capacity, sub_count, 2)),
        ],
        axis=-1,
    )
    meta_width = -(-(local_sub + 2) // 128) * 128
    meta = jnp.pad(meta, ((0, 0), (0, 0), (0, 0), (0, meta_width - local_sub - 2)))
    meta = meta.transpose(0, 2, 1, 3).reshape(owners * sub_count, capacity, meta_width)
    rows = lax.all_to_all(split_rows, ("dom", "sub"), split_axis=0, concat_axis=0, tiled=True)
    meta = lax.all_to_all(meta, ("dom", "sub"), split_axis=0, concat_axis=0, tiled=True)
    rows = rows.reshape(-1, columns)
    meta = meta.reshape(-1, meta_width)

    row_codes = meta[:, :local_sub].astype(jnp.int32)
    id_floats = meta[:, local_sub : local_sub + 2].astype(jnp.float32)
    slot_ids = (id_floats[:, 0] * ID_BASE + id_floats[:, 1]).astype(jnp.int32)
    usable = slot_ids < part_local
    safe_ids = jnp.minimum(slot_ids, part_local - 1)

    same = (slot_ids[:, None] == slot_ids[None, :]) & usable[:, None]
    same_table = same.astype(jnp.bfloat16)
    filled = jnp.sum(same.astype(jnp.float32), axis=1)
    floors = jnp.maximum(filled, 1.0)[:, None]
    sum_x = jnp.dot(same_table, rows, preferred_element_type=jnp.float32)
    as_float = rows.astype(jnp.float32)
    current = jnp.take(centroids, safe_ids, axis=0)
    pick = (safe_ids[:, None] == jnp.arange(part_local, dtype=jnp.int32)[None, :]).astype(jnp.bfloat16)
    weight_fractions = exact_pick(pick, perp_ratio)[:, None]
    filled_fraction = weight_fractions * filled[:, None]
    stats = lax.psum(
        jnp.stack([jnp.sum(as_float * as_float, axis=1), jnp.sum(as_float * current, axis=1)]), "sub"
    )
    norms = stats[0]
    inner = stats[1]
    for iteration in range(ITERS):
        if iteration > 0:
            inner = lax.psum(jnp.sum(as_float * current, axis=1), "sub")
        weight = inner / (norms + 1e-06)
        projected = split_dot(same_table, as_float * weight[:, None])
        current = (
            current
            - (filled_fraction * current + (1.0 - weight_fractions) * projected - sum_x) / floors
        )
    write_ids = jnp.where(usable, slot_ids, part_local)
    new_centroids = centroids.at[write_ids].set(current, mode="drop")
    residual = jnp.where(usable[:, None], as_float - current, 0.0).astype(jnp.bfloat16)

    code_member = (
        (row_codes[:, :, None] == jnp.arange(code_count, dtype=jnp.int32)[None, None, :])
        & usable[:, None, None]
    ).astype(jnp.bfloat16)
    pieces = residual.reshape(-1, local_sub, sub_dim)
    book_sums = jnp.einsum("rmk,rmd->mkd", code_member, pieces, preferred_element_type=jnp.float32)
    book_counts = jnp.sum(code_member, axis=0, dtype=jnp.float32)
    packed = jnp.concatenate([book_sums.reshape(-1), book_counts.reshape(-1)])
    gathered = lax.all_gather(packed.reshape(-1, 128), "dom", axis=0, tiled=False)
    packed = jnp.sum(gathered, axis=0).reshape(-1)
    entries = local_sub * code_count
    totals = packed[: entries * sub_dim].reshape(entries, sub_dim)
    tallies = packed[entries * sub_dim :]
    weights = codeword_weight_total.reshape(entries, 1)
    updated = (codebook.reshape(entries, sub_dim) * weights + totals) / (weights + tallies[:, None])

    outgoing = residual.reshape(owners * sub_count, capacity, columns)
    returned = lax.all_to_all(outgoing, ("dom", "sub"), split_axis=0, concat_axis=0, tiled=True)
    returned = returned.reshape(owners, sub_count, capacity, columns).transpose(0, 2, 1, 3)
    flat_rows = returned.reshape(owners * capacity, row_width)
    residual_rows = jnp.take(flat_rows, slot_index, axis=0)
    return (new_centroids, residual_rows, updated.reshape(local_sub, code_count, sub_dim))


def solution(mesh):
    placed = (
        P(("dom", "sub"), None),
        P(("dom", "sub")),
        P(("dom", "sub"), None),
        P("dom", "sub"),
        P("dom"),
        P("sub", None, None),
        P("sub", None),
    )
    return jax.shard_map(
        per_device,
        mesh=mesh,
        in_specs=placed,
        out_specs=(P("dom", "sub"), P(("dom", "sub"), None), P("sub", None, None)),
        check_vma=False,
    )
```

```python
import jax
import jax.numpy as jnp
from jax import lax
from jax.sharding import PartitionSpec as P

ITERS = 4
ID_BASE = 64


def split_dot(table, values):
    high = lax.reduce_precision(values, exponent_bits=8, mantissa_bits=7)
    low = (values - high).astype(jnp.bfloat16)
    width = values.shape[1]
    parts = jnp.concatenate([high.astype(jnp.bfloat16), low], axis=1)
    both = jnp.dot(table, parts, preferred_element_type=jnp.float32)
    return both[:, :width] + both[:, width:]


def exact_pick(pick, values):
    high = lax.reduce_precision(values, exponent_bits=8, mantissa_bits=7)
    rest = values - high
    middle = lax.reduce_precision(rest, exponent_bits=8, mantissa_bits=7)
    low = rest - middle
    parts = jnp.stack([high, middle, low], axis=1).astype(jnp.bfloat16)
    picked = jnp.dot(pick, parts, preferred_element_type=jnp.float32)
    return (picked[:, 0] + picked[:, 1]) + picked[:, 2]


def shift_sum(values, axis):
    count = lax.axis_size(axis)
    total = values
    for shift in range(1, count):
        pairs = [(source, (source + shift) % count) for source in range(count)]
        total = total + lax.ppermute(values, axis, pairs)
    return total


def ordered_sum(values, axis):
    count = lax.axis_size(axis)
    arrived = [values]
    for shift in range(1, count):
        pairs = [(source, (source + shift) % count) for source in range(count)]
        arrived.append(lax.ppermute(values, axis, pairs))
    stacked = jnp.stack(arrived)
    order = (lax.axis_index(axis) - jnp.arange(count, dtype=jnp.int32)) % count
    return jnp.sum(jnp.take(stacked, order, axis=0), axis=0)


def per_device(vectors, assign, codes, centroids, perp_ratio, codebook, codeword_weight_total):
    owners = lax.axis_size("dom")
    sub_count = lax.axis_size("sub")
    rows_dev, row_width = vectors.shape
    part_local, columns = centroids.shape
    local_sub, code_count, sub_dim = codebook.shape
    capacity = 2 * rows_dev // owners

    owner_of = assign // part_local
    owner_mask = owner_of[:, None] == jnp.arange(owners, dtype=jnp.int32)[None, :]
    counts = jnp.sum(owner_mask.astype(jnp.int32), axis=0)
    starts = jnp.cumsum(counts) - counts
    first_row_index = jnp.sum(jnp.where(owner_mask, starts[None, :], 0), axis=1)
    position = jnp.arange(rows_dev, dtype=jnp.int32) - first_row_index
    slot_index = owner_of * capacity + position
    source_rows = starts[:, None] + jnp.arange(capacity, dtype=jnp.int32)[None, :]
    usable_slot = jnp.arange(capacity, dtype=jnp.int32)[None, :] < counts[:, None]
    clipped = jnp.minimum(source_rows, rows_dev - 1)
    send_rows = jnp.where(
        usable_slot[:, :, None], jnp.take(vectors, clipped, axis=0), jnp.zeros((), jnp.bfloat16)
    )
    send_codes = jnp.take(codes, clipped, axis=0).astype(jnp.bfloat16)
    owner_base = (jnp.arange(owners, dtype=jnp.int32) * part_local)[:, None]
    send_ids = jnp.where(usable_slot, jnp.take(assign, clipped, axis=0) - owner_base, part_local)
    id_parts = jnp.stack([send_ids // ID_BASE, send_ids % ID_BASE], axis=-1).astype(jnp.bfloat16)
    split_rows = send_rows.reshape(owners, capacity, sub_count, columns).transpose(0, 2, 1, 3)
    split_rows = split_rows.reshape(owners * sub_count, capacity, columns)
    meta = jnp.concatenate(
        [
            send_codes.reshape(owners, capacity, sub_count, local_sub),
            jnp.broadcast_to(id_parts[:, :, None, :], (owners, capacity, sub_count, 2)),
        ],
        axis=-1,
    )
    meta_width = -(-(local_sub + 2) // 128) * 128
    meta = jnp.pad(meta, ((0, 0), (0, 0), (0, 0), (0, meta_width - local_sub - 2)))
    meta = meta.transpose(0, 2, 1, 3).reshape(owners * sub_count, capacity, meta_width)
    rows = lax.all_to_all(split_rows, ("dom", "sub"), split_axis=0, concat_axis=0, tiled=True)
    meta = lax.all_to_all(meta, ("dom", "sub"), split_axis=0, concat_axis=0, tiled=True)
    rows = rows.reshape(-1, columns)
    meta = meta.reshape(-1, meta_width)

    row_codes = meta[:, :local_sub].astype(jnp.int32)
    id_floats = meta[:, local_sub : local_sub + 2].astype(jnp.float32)
    slot_ids = (id_floats[:, 0] * ID_BASE + id_floats[:, 1]).astype(jnp.int32)
    usable = slot_ids < part_local
    safe_ids = jnp.minimum(slot_ids, part_local - 1)

    same = (slot_ids[:, None] == slot_ids[None, :]) & usable[:, None]
    same_table = same.astype(jnp.bfloat16)
    filled = jnp.sum(same.astype(jnp.float32), axis=1)
    floors = jnp.maximum(filled, 1.0)[:, None]
    sum_x = jnp.dot(same_table, rows, preferred_element_type=jnp.float32)
    as_float = rows.astype(jnp.float32)
    current = jnp.take(centroids, safe_ids, axis=0)
    pick = (safe_ids[:, None] == jnp.arange(part_local, dtype=jnp.int32)[None, :]).astype(jnp.bfloat16)
    weight_fractions = exact_pick(pick, perp_ratio)[:, None]
    filled_fraction = weight_fractions * filled[:, None]
    stats = shift_sum(
        jnp.stack([jnp.sum(as_float * as_float, axis=1), jnp.sum(as_float * current, axis=1)]), "sub"
    )
    norms = stats[0]
    inner = stats[1]
    for iteration in range(ITERS):
        if iteration > 0:
            inner = shift_sum(jnp.sum(as_float * current, axis=1), "sub")
        weight = inner / (norms + 1e-06)
        projected = split_dot(same_table, as_float * weight[:, None])
        current = (
            current
            - (filled_fraction * current + (1.0 - weight_fractions) * projected - sum_x) / floors
        )
    write_ids = jnp.where(usable, slot_ids, part_local)
    new_centroids = centroids.at[write_ids].set(current, mode="drop")
    residual = jnp.where(usable[:, None], as_float - current, 0.0).astype(jnp.bfloat16)

    code_member = (
        (row_codes[:, :, None] == jnp.arange(code_count, dtype=jnp.int32)[None, None, :])
        & usable[:, None, None]
    ).astype(jnp.bfloat16)
    pieces = residual.reshape(-1, local_sub, sub_dim)
    book_sums = jnp.einsum("rmk,rmd->mkd", code_member, pieces, preferred_element_type=jnp.float32)
    book_counts = jnp.sum(code_member, axis=0, dtype=jnp.float32)
    packed = jnp.concatenate([book_sums.reshape(-1), book_counts.reshape(-1)])
    packed = ordered_sum(packed.reshape(-1, 128), "dom").reshape(-1)
    entries = local_sub * code_count
    totals = packed[: entries * sub_dim].reshape(entries, sub_dim)
    tallies = packed[entries * sub_dim :]
    weights = codeword_weight_total.reshape(entries, 1)
    updated = (codebook.reshape(entries, sub_dim) * weights + totals) / (weights + tallies[:, None])

    outgoing = residual.reshape(owners * sub_count, capacity, columns)
    returned = lax.all_to_all(outgoing, ("dom", "sub"), split_axis=0, concat_axis=0, tiled=True)
    returned = returned.reshape(owners, sub_count, capacity, columns).transpose(0, 2, 1, 3)
    flat_rows = returned.reshape(owners * capacity, row_width)
    residual_rows = jnp.take(flat_rows, slot_index, axis=0)
    return (new_centroids, residual_rows, updated.reshape(local_sub, code_count, sub_dim))


def solution(mesh):
    placed = (
        P(("dom", "sub"), None),
        P(("dom", "sub")),
        P(("dom", "sub"), None),
        P("dom", "sub"),
        P("dom"),
        P("sub", None, None),
        P("sub", None),
    )
    return jax.shard_map(
        per_device,
        mesh=mesh,
        in_specs=placed,
        out_specs=(P("dom", "sub"), P(("dom", "sub"), None), P("sub", None, None)),
        check_vma=False,
    )
```

```python
import jax
import jax.numpy as jnp
from jax import lax
from jax.sharding import PartitionSpec as P

ITERS = 4
ID_BASE = 64


def split_dot(table, values):
    high = lax.reduce_precision(values, exponent_bits=8, mantissa_bits=7)
    low = (values - high).astype(jnp.bfloat16)
    width = values.shape[1]
    parts = jnp.concatenate([high.astype(jnp.bfloat16), low], axis=1)
    both = jnp.dot(table, parts, preferred_element_type=jnp.float32)
    return both[:, :width] + both[:, width:]


def exact_pick(pick, values):
    high = lax.reduce_precision(values, exponent_bits=8, mantissa_bits=7)
    rest = values - high
    middle = lax.reduce_precision(rest, exponent_bits=8, mantissa_bits=7)
    low = rest - middle
    parts = jnp.stack([high, middle, low], axis=1).astype(jnp.bfloat16)
    picked = jnp.dot(pick, parts, preferred_element_type=jnp.float32)
    return (picked[:, 0] + picked[:, 1]) + picked[:, 2]


def shift_sum(values, axis):
    count = lax.axis_size(axis)
    total = values
    for shift in range(1, count):
        pairs = [(source, (source + shift) % count) for source in range(count)]
        total = total + lax.ppermute(values, axis, pairs)
    return total


def ordered_sum(values, axis):
    count = lax.axis_size(axis)
    arrived = [values]
    for shift in range(1, count):
        pairs = [(source, (source + shift) % count) for source in range(count)]
        arrived.append(lax.ppermute(values, axis, pairs))
    stacked = jnp.stack(arrived)
    order = (lax.axis_index(axis) - jnp.arange(count, dtype=jnp.int32)) % count
    return jnp.sum(jnp.take(stacked, order, axis=0), axis=0)


def per_device(vectors, assign, codes, centroids, perp_ratio, codebook, codeword_weight_total):
    owners = lax.axis_size("dom")
    sub_count = lax.axis_size("sub")
    rows_dev, row_width = vectors.shape
    part_local, columns = centroids.shape
    local_sub, code_count, sub_dim = codebook.shape
    capacity = 2 * rows_dev // owners

    owner_of = assign // part_local
    owner_mask = owner_of[:, None] == jnp.arange(owners, dtype=jnp.int32)[None, :]
    counts = jnp.sum(owner_mask.astype(jnp.int32), axis=0)
    starts = jnp.cumsum(counts) - counts
    first_row_index = jnp.sum(jnp.where(owner_mask, starts[None, :], 0), axis=1)
    position = jnp.arange(rows_dev, dtype=jnp.int32) - first_row_index
    slot_index = owner_of * capacity + position
    usable_slot = jnp.arange(capacity, dtype=jnp.int32)[None, :] < counts[:, None]
    def owner_blocks(values):
        padded = jnp.pad(values, ((0, capacity),) + ((0, 0),) * (values.ndim - 1))
        return jnp.stack(
            [lax.dynamic_slice_in_dim(padded, starts[o], capacity, axis=0) for o in range(owners)]
        )

    send_rows = jnp.where(usable_slot[:, :, None], owner_blocks(vectors), jnp.zeros((), jnp.bfloat16))
    send_codes = owner_blocks(codes).astype(jnp.bfloat16)
    owner_base = (jnp.arange(owners, dtype=jnp.int32) * part_local)[:, None]
    send_ids = jnp.where(usable_slot, owner_blocks(assign) - owner_base, part_local)
    id_parts = jnp.stack([send_ids // ID_BASE, send_ids % ID_BASE], axis=-1).astype(jnp.bfloat16)
    meta_width = -(-(local_sub + 2) // 128) * 128
    packet = jnp.concatenate(
        [
            send_rows.reshape(owners, capacity, sub_count, columns),
            send_codes.reshape(owners, capacity, sub_count, local_sub),
            jnp.broadcast_to(id_parts[:, :, None, :], (owners, capacity, sub_count, 2)),
            jnp.zeros((owners, capacity, sub_count, meta_width - local_sub - 2), jnp.bfloat16),
        ],
        axis=-1,
    )
    width = columns + meta_width
    packet = packet.transpose(0, 2, 1, 3).reshape(owners * sub_count, capacity, width)
    arrived = lax.all_to_all(packet, ("dom", "sub"), split_axis=0, concat_axis=0, tiled=True)
    arrived = arrived.reshape(-1, width)
    rows = arrived[:, :columns]
    meta = arrived[:, columns:]

    row_codes = meta[:, :local_sub].astype(jnp.int32)
    id_floats = meta[:, local_sub : local_sub + 2].astype(jnp.float32)
    slot_ids = (id_floats[:, 0] * ID_BASE + id_floats[:, 1]).astype(jnp.int32)
    usable = slot_ids < part_local
    safe_ids = jnp.minimum(slot_ids, part_local - 1)

    same = (slot_ids[:, None] == slot_ids[None, :]) & usable[:, None]
    same_table = same.astype(jnp.bfloat16)
    filled = jnp.sum(same.astype(jnp.float32), axis=1)
    floors = jnp.maximum(filled, 1.0)[:, None]
    sum_x = jnp.dot(same_table, rows, preferred_element_type=jnp.float32)
    as_float = rows.astype(jnp.float32)
    current = jnp.take(centroids, safe_ids, axis=0)
    pick = (safe_ids[:, None] == jnp.arange(part_local, dtype=jnp.int32)[None, :]).astype(jnp.bfloat16)
    weight_fractions = exact_pick(pick, perp_ratio)[:, None]
    filled_fraction = weight_fractions * filled[:, None]
    stats = shift_sum(
        jnp.stack([jnp.sum(as_float * as_float, axis=1), jnp.sum(as_float * current, axis=1)]), "sub"
    )
    norms = stats[0]
    inner = stats[1]
    for iteration in range(ITERS):
        if iteration > 0:
            inner = shift_sum(jnp.sum(as_float * current, axis=1), "sub")
        weight = inner / (norms + 1e-06)
        projected = split_dot(same_table, as_float * weight[:, None])
        current = (
            current
            - (filled_fraction * current + (1.0 - weight_fractions) * projected - sum_x) / floors
        )
    write_ids = jnp.where(usable, slot_ids, part_local)
    new_centroids = centroids.at[write_ids].set(current, mode="drop")
    residual = jnp.where(usable[:, None], as_float - current, 0.0).astype(jnp.bfloat16)

    code_member = (
        (row_codes[:, :, None] == jnp.arange(code_count, dtype=jnp.int32)[None, None, :])
        & usable[:, None, None]
    ).astype(jnp.bfloat16)
    pieces = residual.reshape(-1, local_sub, sub_dim)
    book_sums = jnp.einsum("rmk,rmd->mkd", code_member, pieces, preferred_element_type=jnp.float32)
    book_counts = jnp.sum(code_member, axis=0, dtype=jnp.float32)
    packed = jnp.concatenate([book_sums.reshape(-1), book_counts.reshape(-1)])
    packed = ordered_sum(packed.reshape(-1, 128), "dom").reshape(-1)
    entries = local_sub * code_count
    totals = packed[: entries * sub_dim].reshape(entries, sub_dim)
    tallies = packed[entries * sub_dim :]
    weights = codeword_weight_total.reshape(entries, 1)
    updated = (codebook.reshape(entries, sub_dim) * weights + totals) / (weights + tallies[:, None])

    outgoing = residual.reshape(owners * sub_count, capacity, columns)
    returned = lax.all_to_all(outgoing, ("dom", "sub"), split_axis=0, concat_axis=0, tiled=True)
    returned = returned.reshape(owners, sub_count, capacity, columns).transpose(0, 2, 1, 3)
    flat_rows = returned.reshape(owners * capacity, row_width)
    residual_rows = jnp.take(flat_rows, slot_index, axis=0)
    return (new_centroids, residual_rows, updated.reshape(local_sub, code_count, sub_dim))


def solution(mesh):
    placed = (
        P(("dom", "sub"), None),
        P(("dom", "sub")),
        P(("dom", "sub"), None),
        P("dom", "sub"),
        P("dom"),
        P("sub", None, None),
        P("sub", None),
    )
    return jax.shard_map(
        per_device,
        mesh=mesh,
        in_specs=placed,
        out_specs=(P("dom", "sub"), P(("dom", "sub"), None), P("sub", None, None)),
        check_vma=False,
    )
```

```python
import jax
import jax.numpy as jnp
from jax import lax
from jax.sharding import PartitionSpec as P

ITERS = 4
ID_BASE = 64


def split_dot(table, values):
    high = lax.reduce_precision(values, exponent_bits=8, mantissa_bits=7)
    low = (values - high).astype(jnp.bfloat16)
    width = values.shape[1]
    parts = jnp.concatenate([high.astype(jnp.bfloat16), low], axis=1)
    both = jnp.dot(table, parts, preferred_element_type=jnp.float32)
    return both[:, :width] + both[:, width:]


def exact_pick(pick_hi, pick_lo, table):
    high = lax.reduce_precision(table, exponent_bits=8, mantissa_bits=7)
    rest = table - high
    middle = lax.reduce_precision(rest, exponent_bits=8, mantissa_bits=7)
    low = rest - middle
    lanes = table.shape[1]
    parts = jnp.concatenate([high, middle, low], axis=1).astype(jnp.bfloat16)
    picked = jnp.dot(pick_hi, parts, preferred_element_type=jnp.float32)
    chosen = [
        jnp.sum(jnp.where(pick_lo, picked[:, k * lanes : (k + 1) * lanes], 0.0), axis=1) for k in range(3)
    ]
    return (chosen[0] + chosen[1]) + chosen[2]


def shift_sum(values, axis):
    count = lax.axis_size(axis)
    total = values
    for shift in range(1, count):
        pairs = [(source, (source + shift) % count) for source in range(count)]
        total = total + lax.ppermute(values, axis, pairs)
    return total


def ordered_sum(values, axis):
    count = lax.axis_size(axis)
    arrived = [values]
    for shift in range(1, count):
        pairs = [(source, (source + shift) % count) for source in range(count)]
        arrived.append(lax.ppermute(values, axis, pairs))
    stacked = jnp.stack(arrived)
    order = (lax.axis_index(axis) - jnp.arange(count, dtype=jnp.int32)) % count
    return jnp.sum(jnp.take(stacked, order, axis=0), axis=0)


def per_device(vectors, assign, codes, centroids, perp_ratio, codebook, codeword_weight_total):
    owners = lax.axis_size("dom")
    sub_count = lax.axis_size("sub")
    rows_dev, row_width = vectors.shape
    part_local, columns = centroids.shape
    local_sub, code_count, sub_dim = codebook.shape
    capacity = 2 * rows_dev // owners

    owner_of = assign // part_local
    owner_mask = owner_of[:, None] == jnp.arange(owners, dtype=jnp.int32)[None, :]
    counts = jnp.sum(owner_mask.astype(jnp.int32), axis=0)
    starts = jnp.cumsum(counts) - counts
    first_row_index = jnp.sum(jnp.where(owner_mask, starts[None, :], 0), axis=1)
    position = jnp.arange(rows_dev, dtype=jnp.int32) - first_row_index
    slot_index = owner_of * capacity + position
    source_rows = starts[:, None] + jnp.arange(capacity, dtype=jnp.int32)[None, :]
    usable_slot = jnp.arange(capacity, dtype=jnp.int32)[None, :] < counts[:, None]
    clipped = jnp.minimum(source_rows, rows_dev - 1)
    send_rows = jnp.where(
        usable_slot[:, :, None], jnp.take(vectors, clipped, axis=0), jnp.zeros((), jnp.bfloat16)
    )
    send_codes = jnp.take(codes, clipped, axis=0).astype(jnp.bfloat16)
    owner_base = (jnp.arange(owners, dtype=jnp.int32) * part_local)[:, None]
    send_ids = jnp.where(usable_slot, jnp.take(assign, clipped, axis=0) - owner_base, part_local)
    id_parts = jnp.stack([send_ids // ID_BASE, send_ids % ID_BASE], axis=-1).astype(jnp.bfloat16)
    split_rows = send_rows.reshape(owners, capacity, sub_count, columns).transpose(0, 2, 1, 3)
    split_rows = split_rows.reshape(owners * sub_count, capacity, columns)
    meta = jnp.concatenate(
        [
            send_codes.reshape(owners, capacity, sub_count, local_sub),
            jnp.broadcast_to(id_parts[:, :, None, :], (owners, capacity, sub_count, 2)),
        ],
        axis=-1,
    )
    meta_width = -(-(local_sub + 2) // 128) * 128
    meta = jnp.pad(meta, ((0, 0), (0, 0), (0, 0), (0, meta_width - local_sub - 2)))
    meta = meta.transpose(0, 2, 1, 3).reshape(owners * sub_count, capacity, meta_width)
    rows = lax.all_to_all(split_rows, ("dom", "sub"), split_axis=0, concat_axis=0, tiled=True)
    meta = lax.all_to_all(meta, ("dom", "sub"), split_axis=0, concat_axis=0, tiled=True)
    rows = rows.reshape(-1, columns)
    meta = meta.reshape(-1, meta_width)

    row_codes = meta[:, :local_sub].astype(jnp.int32)
    id_floats = meta[:, local_sub : local_sub + 2].astype(jnp.float32)
    slot_ids = (id_floats[:, 0] * ID_BASE + id_floats[:, 1]).astype(jnp.int32)
    usable = slot_ids < part_local
    safe_ids = jnp.minimum(slot_ids, part_local - 1)

    same = (slot_ids[:, None] == slot_ids[None, :]) & usable[:, None]
    same_table = same.astype(jnp.bfloat16)
    filled = jnp.sum(same.astype(jnp.float32), axis=1)
    floors = jnp.maximum(filled, 1.0)[:, None]
    sum_x = jnp.dot(same_table, rows, preferred_element_type=jnp.float32)
    as_float = rows.astype(jnp.float32)
    current = jnp.take(centroids, safe_ids, axis=0)
    start_rows = current
    digit_hi = id_floats[:, 0].astype(jnp.int32)
    digit_lo = id_floats[:, 1].astype(jnp.int32)
    block_count = part_local // ID_BASE
    pick_hi = (digit_hi[:, None] == jnp.arange(block_count, dtype=jnp.int32)[None, :]).astype(jnp.bfloat16)
    pick_lo = digit_lo[:, None] == jnp.arange(ID_BASE, dtype=jnp.int32)[None, :]
    weight_fractions = exact_pick(pick_hi, pick_lo, perp_ratio.reshape(block_count, ID_BASE))[:, None]
    filled_fraction = weight_fractions * filled[:, None]
    stats = shift_sum(
        jnp.stack([jnp.sum(as_float * as_float, axis=1), jnp.sum(as_float * current, axis=1)]), "sub"
    )
    norms = stats[0]
    inner = stats[1]
    for iteration in range(ITERS):
        if iteration > 0:
            inner = shift_sum(jnp.sum(as_float * current, axis=1), "sub")
        weight = inner / (norms + 1e-06)
        projected = split_dot(same_table, as_float * weight[:, None])
        current = (
            current
            - (filled_fraction * current + (1.0 - weight_fractions) * projected - sum_x) / floors
        )
    slots = slot_ids.shape[0]
    earlier = jnp.arange(slots, dtype=jnp.int32)[None, :] < jnp.arange(slots, dtype=jnp.int32)[:, None]
    first_of_partition = usable & ~jnp.any(same & earlier, axis=1)
    place = (jnp.arange(part_local, dtype=jnp.int32)[:, None] == slot_ids[None, :]) & first_of_partition[None, :]
    new_centroids = centroids + split_dot(place.astype(jnp.bfloat16), current - start_rows)
    residual = jnp.where(usable[:, None], as_float - current, 0.0).astype(jnp.bfloat16)

    code_member = (
        (row_codes[:, :, None] == jnp.arange(code_count, dtype=jnp.int32)[None, None, :])
        & usable[:, None, None]
    ).astype(jnp.bfloat16)
    pieces = residual.reshape(-1, local_sub, sub_dim)
    book_sums = jnp.einsum("rmk,rmd->mkd", code_member, pieces, preferred_element_type=jnp.float32)
    book_counts = jnp.sum(code_member, axis=0, dtype=jnp.float32)
    packed = jnp.concatenate([book_sums.reshape(-1), book_counts.reshape(-1)])
    packed = ordered_sum(packed.reshape(-1, 128), "dom").reshape(-1)
    entries = local_sub * code_count
    totals = packed[: entries * sub_dim].reshape(entries, sub_dim)
    tallies = packed[entries * sub_dim :]
    weights = codeword_weight_total.reshape(entries, 1)
    updated = (codebook.reshape(entries, sub_dim) * weights + totals) / (weights + tallies[:, None])

    outgoing = residual.reshape(owners * sub_count, capacity, columns)
    returned = lax.all_to_all(outgoing, ("dom", "sub"), split_axis=0, concat_axis=0, tiled=True)
    returned = returned.reshape(owners, sub_count, capacity, columns).transpose(0, 2, 1, 3)
    flat_rows = returned.reshape(owners * capacity, row_width)
    residual_rows = jnp.take(flat_rows, slot_index, axis=0)
    return (new_centroids, residual_rows, updated.reshape(local_sub, code_count, sub_dim))


def solution(mesh):
    placed = (
        P(("dom", "sub"), None),
        P(("dom", "sub")),
        P(("dom", "sub"), None),
        P("dom", "sub"),
        P("dom"),
        P("sub", None, None),
        P("sub", None),
    )
    return jax.shard_map(
        per_device,
        mesh=mesh,
        in_specs=placed,
        out_specs=(P("dom", "sub"), P(("dom", "sub"), None), P("sub", None, None)),
        check_vma=False,
    )
```

```python
import jax
import jax.numpy as jnp
from jax import lax
from jax.sharding import PartitionSpec as P

ITERS = 4
ID_BASE = 64


def split_dot(table, values):
    high = lax.reduce_precision(values, exponent_bits=8, mantissa_bits=7)
    low = (values - high).astype(jnp.bfloat16)
    width = values.shape[1]
    parts = jnp.concatenate([high.astype(jnp.bfloat16), low], axis=1)
    both = jnp.dot(table, parts, preferred_element_type=jnp.float32)
    return both[:, :width] + both[:, width:]


def exact_pick(pick_hi, pick_lo, table):
    high = lax.reduce_precision(table, exponent_bits=8, mantissa_bits=7)
    rest = table - high
    middle = lax.reduce_precision(rest, exponent_bits=8, mantissa_bits=7)
    low = rest - middle
    lanes = table.shape[1]
    parts = jnp.concatenate([high, middle, low], axis=1).astype(jnp.bfloat16)
    picked = jnp.dot(pick_hi, parts, preferred_element_type=jnp.float32)
    chosen = [
        jnp.sum(jnp.where(pick_lo, picked[:, k * lanes : (k + 1) * lanes], 0.0), axis=1) for k in range(3)
    ]
    return (chosen[0] + chosen[1]) + chosen[2]


def shift_sum(values, axis):
    count = lax.axis_size(axis)
    total = values
    for shift in range(1, count):
        pairs = [(source, (source + shift) % count) for source in range(count)]
        total = total + lax.ppermute(values, axis, pairs)
    return total


def ordered_sum(values, axis):
    count = lax.axis_size(axis)
    arrived = [values]
    for shift in range(1, count):
        pairs = [(source, (source + shift) % count) for source in range(count)]
        arrived.append(lax.ppermute(values, axis, pairs))
    stacked = jnp.stack(arrived)
    order = (lax.axis_index(axis) - jnp.arange(count, dtype=jnp.int32)) % count
    return jnp.sum(jnp.take(stacked, order, axis=0), axis=0)


def per_device(vectors, assign, codes, centroids, perp_ratio, codebook, codeword_weight_total):
    owners = lax.axis_size("dom")
    sub_count = lax.axis_size("sub")
    rows_dev, row_width = vectors.shape
    part_local, columns = centroids.shape
    local_sub, code_count, sub_dim = codebook.shape
    capacity = 2 * rows_dev // owners

    owner_of = assign // part_local
    owner_mask = owner_of[:, None] == jnp.arange(owners, dtype=jnp.int32)[None, :]
    counts = jnp.sum(owner_mask.astype(jnp.int32), axis=0)
    starts = jnp.cumsum(counts) - counts
    first_row_index = jnp.sum(jnp.where(owner_mask, starts[None, :], 0), axis=1)
    position = jnp.arange(rows_dev, dtype=jnp.int32) - first_row_index
    slot_index = owner_of * capacity + position
    source_rows = starts[:, None] + jnp.arange(capacity, dtype=jnp.int32)[None, :]
    usable_slot = jnp.arange(capacity, dtype=jnp.int32)[None, :] < counts[:, None]
    clipped = jnp.minimum(source_rows, rows_dev - 1)
    send_rows = jnp.where(
        usable_slot[:, :, None], jnp.take(vectors, clipped, axis=0), jnp.zeros((), jnp.bfloat16)
    )
    send_codes = jnp.take(codes, clipped, axis=0).astype(jnp.bfloat16)
    owner_base = (jnp.arange(owners, dtype=jnp.int32) * part_local)[:, None]
    send_ids = jnp.where(usable_slot, jnp.take(assign, clipped, axis=0) - owner_base, part_local)
    id_parts = jnp.stack([send_ids // ID_BASE, send_ids % ID_BASE], axis=-1).astype(jnp.bfloat16)
    split_rows = send_rows.reshape(owners, capacity, sub_count, columns).transpose(0, 2, 1, 3)
    split_rows = split_rows.reshape(owners * sub_count, capacity, columns)
    meta = jnp.concatenate(
        [
            send_codes.reshape(owners, capacity, sub_count, local_sub),
            jnp.broadcast_to(id_parts[:, :, None, :], (owners, capacity, sub_count, 2)),
        ],
        axis=-1,
    )
    meta_width = -(-(local_sub + 2) // 128) * 128
    meta = jnp.pad(meta, ((0, 0), (0, 0), (0, 0), (0, meta_width - local_sub - 2)))
    meta = meta.transpose(0, 2, 1, 3).reshape(owners * sub_count, capacity, meta_width)
    rows = lax.all_to_all(split_rows, ("dom", "sub"), split_axis=0, concat_axis=0, tiled=True)
    meta = lax.all_to_all(meta, ("dom", "sub"), split_axis=0, concat_axis=0, tiled=True)
    rows = rows.reshape(-1, columns)
    meta = meta.reshape(-1, meta_width)

    row_codes = meta[:, :local_sub].astype(jnp.int32)
    id_floats = meta[:, local_sub : local_sub + 2].astype(jnp.float32)
    slot_ids = (id_floats[:, 0] * ID_BASE + id_floats[:, 1]).astype(jnp.int32)
    usable = slot_ids < part_local
    safe_ids = jnp.minimum(slot_ids, part_local - 1)

    same = (slot_ids[:, None] == slot_ids[None, :]) & usable[:, None]
    same_table = same.astype(jnp.bfloat16)
    filled = jnp.sum(same.astype(jnp.float32), axis=1)
    floors = jnp.maximum(filled, 1.0)[:, None]
    sum_x = jnp.dot(same_table, rows, preferred_element_type=jnp.float32)
    as_float = rows.astype(jnp.float32)
    current = jnp.take(centroids, safe_ids, axis=0)
    digit_hi = id_floats[:, 0].astype(jnp.int32)
    digit_lo = id_floats[:, 1].astype(jnp.int32)
    block_count = part_local // ID_BASE
    pick_hi = (digit_hi[:, None] == jnp.arange(block_count, dtype=jnp.int32)[None, :]).astype(jnp.bfloat16)
    pick_lo = digit_lo[:, None] == jnp.arange(ID_BASE, dtype=jnp.int32)[None, :]
    weight_fractions = exact_pick(pick_hi, pick_lo, perp_ratio.reshape(block_count, ID_BASE))[:, None]
    filled_fraction = weight_fractions * filled[:, None]
    stats = shift_sum(
        jnp.stack([jnp.sum(as_float * as_float, axis=1), jnp.sum(as_float * current, axis=1)]), "sub"
    )
    norms = stats[0]
    inner = stats[1]
    for iteration in range(ITERS):
        if iteration > 0:
            inner = shift_sum(jnp.sum(as_float * current, axis=1), "sub")
        weight = inner / (norms + 1e-06)
        projected = split_dot(same_table, as_float * weight[:, None])
        current = (
            current
            - (filled_fraction * current + (1.0 - weight_fractions) * projected - sum_x) / floors
        )
    write_ids = jnp.where(usable, slot_ids, part_local)
    new_centroids = centroids.at[write_ids].set(current, mode="drop")
    residual = jnp.where(usable[:, None], as_float - current, 0.0).astype(jnp.bfloat16)

    code_member = (
        (row_codes[:, :, None] == jnp.arange(code_count, dtype=jnp.int32)[None, None, :])
        & usable[:, None, None]
    ).astype(jnp.bfloat16)
    pieces = residual.reshape(-1, local_sub, sub_dim)
    book_sums = jnp.einsum("rmk,rmd->mkd", code_member, pieces, preferred_element_type=jnp.float32)
    book_counts = jnp.sum(code_member, axis=0, dtype=jnp.float32)
    packed = jnp.concatenate([book_sums.reshape(-1), book_counts.reshape(-1)])
    packed = ordered_sum(packed.reshape(-1, 128), "dom").reshape(-1)
    entries = local_sub * code_count
    totals = packed[: entries * sub_dim].reshape(entries, sub_dim)
    tallies = packed[entries * sub_dim :]
    weights = codeword_weight_total.reshape(entries, 1)
    updated = (codebook.reshape(entries, sub_dim) * weights + totals) / (weights + tallies[:, None])

    outgoing = residual.reshape(owners * sub_count, capacity, columns)
    returned = lax.all_to_all(outgoing, ("dom", "sub"), split_axis=0, concat_axis=0, tiled=True)
    returned = returned.reshape(owners, sub_count, capacity, columns).transpose(0, 2, 1, 3)
    flat_rows = returned.reshape(owners * capacity, row_width)
    residual_rows = jnp.take(flat_rows, slot_index, axis=0)
    return (new_centroids, residual_rows, updated.reshape(local_sub, code_count, sub_dim))


def solution(mesh):
    placed = (
        P(("dom", "sub"), None),
        P(("dom", "sub")),
        P(("dom", "sub"), None),
        P("dom", "sub"),
        P("dom"),
        P("sub", None, None),
        P("sub", None),
    )
    return jax.shard_map(
        per_device,
        mesh=mesh,
        in_specs=placed,
        out_specs=(P("dom", "sub"), P(("dom", "sub"), None), P("sub", None, None)),
        check_vma=False,
    )
```

```python
import jax
import jax.numpy as jnp
from jax import lax
from jax.sharding import PartitionSpec as P

ITERS = 4
ID_BASE = 64


def split_dot(table, values):
    high = lax.reduce_precision(values, exponent_bits=8, mantissa_bits=7)
    low = (values - high).astype(jnp.bfloat16)
    width = values.shape[1]
    parts = jnp.concatenate([high.astype(jnp.bfloat16), low], axis=1)
    both = jnp.dot(table, parts, preferred_element_type=jnp.float32)
    return both[:, :width] + both[:, width:]


def exact_pick(pick_hi, pick_lo, table):
    high = lax.reduce_precision(table, exponent_bits=8, mantissa_bits=7)
    rest = table - high
    middle = lax.reduce_precision(rest, exponent_bits=8, mantissa_bits=7)
    low = rest - middle
    lanes = table.shape[1]
    parts = jnp.concatenate([high, middle, low], axis=1).astype(jnp.bfloat16)
    picked = jnp.dot(pick_hi, parts, preferred_element_type=jnp.float32)
    chosen = [
        jnp.sum(jnp.where(pick_lo, picked[:, k * lanes : (k + 1) * lanes], 0.0), axis=1) for k in range(3)
    ]
    return (chosen[0] + chosen[1]) + chosen[2]


def shift_sum(values, axis):
    count = lax.axis_size(axis)
    total = values
    for shift in range(1, count):
        pairs = [(source, (source + shift) % count) for source in range(count)]
        total = total + lax.ppermute(values, axis, pairs)
    return total


def ordered_sum(values, axis):
    count = lax.axis_size(axis)
    arrived = [values]
    for shift in range(1, count):
        pairs = [(source, (source + shift) % count) for source in range(count)]
        arrived.append(lax.ppermute(values, axis, pairs))
    stacked = jnp.stack(arrived)
    order = (lax.axis_index(axis) - jnp.arange(count, dtype=jnp.int32)) % count
    return jnp.sum(jnp.take(stacked, order, axis=0), axis=0)


def per_device(vectors, assign, codes, centroids, perp_ratio, codebook, codeword_weight_total):
    owners = lax.axis_size("dom")
    sub_count = lax.axis_size("sub")
    rows_dev, row_width = vectors.shape
    part_local, columns = centroids.shape
    local_sub, code_count, sub_dim = codebook.shape
    capacity = 2 * rows_dev // owners

    owner_of = assign // part_local
    owner_mask = owner_of[:, None] == jnp.arange(owners, dtype=jnp.int32)[None, :]
    counts = jnp.sum(owner_mask.astype(jnp.int32), axis=0)
    starts = jnp.cumsum(counts) - counts
    first_row_index = jnp.sum(jnp.where(owner_mask, starts[None, :], 0), axis=1)
    position = jnp.arange(rows_dev, dtype=jnp.int32) - first_row_index
    slot_index = owner_of * capacity + position
    source_rows = starts[:, None] + jnp.arange(capacity, dtype=jnp.int32)[None, :]
    usable_slot = jnp.arange(capacity, dtype=jnp.int32)[None, :] < counts[:, None]
    clipped = jnp.minimum(source_rows, rows_dev - 1)
    send_rows = jnp.where(
        usable_slot[:, :, None], jnp.take(vectors, clipped, axis=0), jnp.zeros((), jnp.bfloat16)
    )
    send_codes = jnp.take(codes, clipped, axis=0).astype(jnp.bfloat16)
    owner_base = (jnp.arange(owners, dtype=jnp.int32) * part_local)[:, None]
    send_ids = jnp.where(usable_slot, jnp.take(assign, clipped, axis=0) - owner_base, part_local)
    id_parts = jnp.stack([send_ids // ID_BASE, send_ids % ID_BASE], axis=-1).astype(jnp.bfloat16)
    split_rows = send_rows.reshape(owners, capacity, sub_count, columns).transpose(0, 2, 1, 3)
    split_rows = split_rows.reshape(owners * sub_count, capacity, columns)
    meta = jnp.concatenate(
        [
            send_codes.reshape(owners, capacity, sub_count, local_sub),
            jnp.broadcast_to(id_parts[:, :, None, :], (owners, capacity, sub_count, 2)),
        ],
        axis=-1,
    )
    meta_width = local_sub + 2
    extra_rows = -(-(capacity * meta_width) // columns)
    meta = meta.transpose(0, 2, 1, 3).reshape(owners * sub_count, capacity * meta_width)
    meta = jnp.pad(meta, ((0, 0), (0, extra_rows * columns - capacity * meta_width)))
    packet = jnp.concatenate([split_rows, meta.reshape(owners * sub_count, extra_rows, columns)], axis=1)
    arrived = lax.all_to_all(packet, ("dom", "sub"), split_axis=0, concat_axis=0, tiled=True)
    rows = arrived[:, :capacity].reshape(-1, columns)
    meta = arrived[:, capacity:].reshape(owners * sub_count, extra_rows * columns)
    meta = meta[:, : capacity * meta_width].reshape(-1, meta_width)

    row_codes = meta[:, :local_sub].astype(jnp.int32)
    id_floats = meta[:, local_sub : local_sub + 2].astype(jnp.float32)
    slot_ids = (id_floats[:, 0] * ID_BASE + id_floats[:, 1]).astype(jnp.int32)
    usable = slot_ids < part_local
    safe_ids = jnp.minimum(slot_ids, part_local - 1)

    same = (slot_ids[:, None] == slot_ids[None, :]) & usable[:, None]
    same_table = same.astype(jnp.bfloat16)
    filled = jnp.sum(same.astype(jnp.float32), axis=1)
    floors = jnp.maximum(filled, 1.0)[:, None]
    sum_x = jnp.dot(same_table, rows, preferred_element_type=jnp.float32)
    as_float = rows.astype(jnp.float32)
    current = jnp.take(centroids, safe_ids, axis=0)
    digit_hi = id_floats[:, 0].astype(jnp.int32)
    digit_lo = id_floats[:, 1].astype(jnp.int32)
    block_count = part_local // ID_BASE
    pick_hi = (digit_hi[:, None] == jnp.arange(block_count, dtype=jnp.int32)[None, :]).astype(jnp.bfloat16)
    pick_lo = digit_lo[:, None] == jnp.arange(ID_BASE, dtype=jnp.int32)[None, :]
    weight_fractions = exact_pick(pick_hi, pick_lo, perp_ratio.reshape(block_count, ID_BASE))[:, None]
    filled_fraction = weight_fractions * filled[:, None]
    stats = shift_sum(
        jnp.stack([jnp.sum(as_float * as_float, axis=1), jnp.sum(as_float * current, axis=1)]), "sub"
    )
    norms = stats[0]
    inner = stats[1]
    for iteration in range(ITERS):
        if iteration > 0:
            inner = shift_sum(jnp.sum(as_float * current, axis=1), "sub")
        weight = inner / (norms + 1e-06)
        projected = split_dot(same_table, as_float * weight[:, None])
        current = (
            current
            - (filled_fraction * current + (1.0 - weight_fractions) * projected - sum_x) / floors
        )
    write_ids = jnp.where(usable, slot_ids, part_local)
    new_centroids = centroids.at[write_ids].set(current, mode="drop")
    residual = jnp.where(usable[:, None], as_float - current, 0.0).astype(jnp.bfloat16)

    code_member = (
        (row_codes[:, :, None] == jnp.arange(code_count, dtype=jnp.int32)[None, None, :])
        & usable[:, None, None]
    ).astype(jnp.bfloat16)
    pieces = residual.reshape(-1, local_sub, sub_dim)
    book_sums = jnp.einsum("rmk,rmd->mkd", code_member, pieces, preferred_element_type=jnp.float32)
    book_counts = jnp.sum(code_member, axis=0, dtype=jnp.float32)
    packed = jnp.concatenate([book_sums.reshape(-1), book_counts.reshape(-1)])
    packed = ordered_sum(packed.reshape(-1, 128), "dom").reshape(-1)
    entries = local_sub * code_count
    totals = packed[: entries * sub_dim].reshape(entries, sub_dim)
    tallies = packed[entries * sub_dim :]
    weights = codeword_weight_total.reshape(entries, 1)
    updated = (codebook.reshape(entries, sub_dim) * weights + totals) / (weights + tallies[:, None])

    outgoing = residual.reshape(owners * sub_count, capacity, columns)
    returned = lax.all_to_all(outgoing, ("dom", "sub"), split_axis=0, concat_axis=0, tiled=True)
    returned = returned.reshape(owners, sub_count, capacity, columns).transpose(0, 2, 1, 3)
    flat_rows = returned.reshape(owners * capacity, row_width)
    residual_rows = jnp.take(flat_rows, slot_index, axis=0)
    return (new_centroids, residual_rows, updated.reshape(local_sub, code_count, sub_dim))


def solution(mesh):
    placed = (
        P(("dom", "sub"), None),
        P(("dom", "sub")),
        P(("dom", "sub"), None),
        P("dom", "sub"),
        P("dom"),
        P("sub", None, None),
        P("sub", None),
    )
    return jax.shard_map(
        per_device,
        mesh=mesh,
        in_specs=placed,
        out_specs=(P("dom", "sub"), P(("dom", "sub"), None), P("sub", None, None)),
        check_vma=False,
    )
```

```python
import jax
import jax.numpy as jnp
from jax import lax
from jax.sharding import PartitionSpec as P

ITERS = 4
ID_BASE = 64


def split_dot(table, values):
    high = lax.reduce_precision(values, exponent_bits=8, mantissa_bits=7)
    low = (values - high).astype(jnp.bfloat16)
    width = values.shape[1]
    parts = jnp.concatenate([high.astype(jnp.bfloat16), low], axis=1)
    both = jnp.dot(table, parts, preferred_element_type=jnp.float32)
    return both[:, :width] + both[:, width:]


def exact_pick(pick_hi, pick_lo, table):
    high = lax.reduce_precision(table, exponent_bits=8, mantissa_bits=7)
    rest = table - high
    middle = lax.reduce_precision(rest, exponent_bits=8, mantissa_bits=7)
    low = rest - middle
    lanes = table.shape[1]
    parts = jnp.concatenate([high, middle, low], axis=1).astype(jnp.bfloat16)
    picked = jnp.dot(pick_hi, parts, preferred_element_type=jnp.float32)
    chosen = [
        jnp.sum(jnp.where(pick_lo, picked[:, k * lanes : (k + 1) * lanes], 0.0), axis=1) for k in range(3)
    ]
    return (chosen[0] + chosen[1]) + chosen[2]


def shift_sum(values, axis):
    count = lax.axis_size(axis)
    total = values
    for shift in range(1, count):
        pairs = [(source, (source + shift) % count) for source in range(count)]
        total = total + lax.ppermute(values, axis, pairs)
    return total


def ordered_sum(values, axis):
    count = lax.axis_size(axis)
    arrived = [values]
    for shift in range(1, count):
        pairs = [(source, (source + shift) % count) for source in range(count)]
        arrived.append(lax.ppermute(values, axis, pairs))
    stacked = jnp.stack(arrived)
    order = (lax.axis_index(axis) - jnp.arange(count, dtype=jnp.int32)) % count
    return jnp.sum(jnp.take(stacked, order, axis=0), axis=0)


def per_device(vectors, assign, codes, centroids, perp_ratio, codebook, codeword_weight_total):
    owners = lax.axis_size("dom")
    sub_count = lax.axis_size("sub")
    rows_dev, row_width = vectors.shape
    part_local, columns = centroids.shape
    local_sub, code_count, sub_dim = codebook.shape
    capacity = 2 * rows_dev // owners

    owner_of = assign // part_local
    owner_mask = owner_of[:, None] == jnp.arange(owners, dtype=jnp.int32)[None, :]
    counts = jnp.sum(owner_mask.astype(jnp.int32), axis=0)
    starts = jnp.cumsum(counts) - counts
    first_row_index = jnp.sum(jnp.where(owner_mask, starts[None, :], 0), axis=1)
    position = jnp.arange(rows_dev, dtype=jnp.int32) - first_row_index
    slot_index = owner_of * capacity + position
    source_rows = starts[:, None] + jnp.arange(capacity, dtype=jnp.int32)[None, :]
    usable_slot = jnp.arange(capacity, dtype=jnp.int32)[None, :] < counts[:, None]
    clipped = jnp.minimum(source_rows, rows_dev - 1)
    send_rows = jnp.where(
        usable_slot[:, :, None], jnp.take(vectors, clipped, axis=0), jnp.zeros((), jnp.bfloat16)
    )
    send_codes = jnp.take(codes, clipped, axis=0).astype(jnp.bfloat16)
    owner_base = (jnp.arange(owners, dtype=jnp.int32) * part_local)[:, None]
    send_ids = jnp.where(usable_slot, jnp.take(assign, clipped, axis=0) - owner_base, part_local)
    id_parts = jnp.stack([send_ids // ID_BASE, send_ids % ID_BASE], axis=-1).astype(jnp.bfloat16)
    split_rows = send_rows.reshape(owners, capacity, sub_count, columns).transpose(0, 2, 1, 3)
    split_rows = split_rows.reshape(owners * sub_count, capacity, columns)
    meta = jnp.concatenate(
        [
            send_codes.reshape(owners, capacity, sub_count, local_sub),
            jnp.broadcast_to(id_parts[:, :, None, :], (owners, capacity, sub_count, 2)),
        ],
        axis=-1,
    )
    meta_width = -(-(local_sub + 2) // 128) * 128
    meta = jnp.pad(meta, ((0, 0), (0, 0), (0, 0), (0, meta_width - local_sub - 2)))
    meta = meta.transpose(0, 2, 1, 3).reshape(owners * sub_count, capacity, meta_width)
    rows = lax.all_to_all(split_rows, ("dom", "sub"), split_axis=0, concat_axis=0, tiled=True)
    meta = lax.all_to_all(meta, ("dom", "sub"), split_axis=0, concat_axis=0, tiled=True)
    rows = rows.reshape(-1, columns)
    meta = meta.reshape(-1, meta_width)

    row_codes = meta[:, :local_sub].astype(jnp.int32)
    id_floats = meta[:, local_sub : local_sub + 2].astype(jnp.float32)
    slot_ids = (id_floats[:, 0] * ID_BASE + id_floats[:, 1]).astype(jnp.int32)
    usable = slot_ids < part_local
    safe_ids = jnp.minimum(slot_ids, part_local - 1)

    same = (slot_ids[:, None] == slot_ids[None, :]) & usable[:, None]
    same_table = same.astype(jnp.bfloat16)
    filled = jnp.sum(same.astype(jnp.float32), axis=1)
    floors = jnp.maximum(filled, 1.0)[:, None]
    sum_x = jnp.dot(same_table, rows, preferred_element_type=jnp.float32)
    as_float = rows.astype(jnp.float32)
    current = jnp.take(centroids, safe_ids, axis=0)
    digit_hi = id_floats[:, 0].astype(jnp.int32)
    digit_lo = id_floats[:, 1].astype(jnp.int32)
    block_count = part_local // ID_BASE
    pick_hi = (digit_hi[:, None] == jnp.arange(block_count, dtype=jnp.int32)[None, :]).astype(jnp.bfloat16)
    pick_lo = digit_lo[:, None] == jnp.arange(ID_BASE, dtype=jnp.int32)[None, :]
    weight_fractions = exact_pick(pick_hi, pick_lo, perp_ratio.reshape(block_count, ID_BASE))[:, None]
    filled_fraction = weight_fractions * filled[:, None]
    stats = shift_sum(
        jnp.stack([jnp.sum(as_float * as_float, axis=1), jnp.sum(as_float * current, axis=1)]), "sub"
    )
    norms = stats[0]
    inner = stats[1]
    for iteration in range(ITERS):
        if iteration > 0:
            inner = shift_sum(jnp.sum(as_float * current, axis=1), "sub")
        weight = inner / (norms + 1e-06)
        projected = split_dot(same_table, as_float * weight[:, None])
        current = (
            current
            - (filled_fraction * current + (1.0 - weight_fractions) * projected - sum_x) / floors
        )
    write_ids = jnp.where(usable, slot_ids, part_local)
    target = centroids + (meta[0, 0] * 0).astype(jnp.float32)
    new_centroids = target.at[write_ids].set(current, mode="drop")
    residual = jnp.where(usable[:, None], as_float - current, 0.0).astype(jnp.bfloat16)

    code_member = (
        (row_codes[:, :, None] == jnp.arange(code_count, dtype=jnp.int32)[None, None, :])
        & usable[:, None, None]
    ).astype(jnp.bfloat16)
    pieces = residual.reshape(-1, local_sub, sub_dim)
    book_sums = jnp.einsum("rmk,rmd->mkd", code_member, pieces, preferred_element_type=jnp.float32)
    book_counts = jnp.sum(code_member, axis=0, dtype=jnp.float32)
    packed = jnp.concatenate([book_sums.reshape(-1), book_counts.reshape(-1)])
    packed = ordered_sum(packed.reshape(-1, 128), "dom").reshape(-1)
    entries = local_sub * code_count
    totals = packed[: entries * sub_dim].reshape(entries, sub_dim)
    tallies = packed[entries * sub_dim :]
    weights = codeword_weight_total.reshape(entries, 1)
    updated = (codebook.reshape(entries, sub_dim) * weights + totals) / (weights + tallies[:, None])

    outgoing = residual.reshape(owners * sub_count, capacity, columns)
    returned = lax.all_to_all(outgoing, ("dom", "sub"), split_axis=0, concat_axis=0, tiled=True)
    returned = returned.reshape(owners, sub_count, capacity, columns).transpose(0, 2, 1, 3)
    flat_rows = returned.reshape(owners * capacity, row_width)
    residual_rows = jnp.take(flat_rows, slot_index, axis=0)
    return (new_centroids, residual_rows, updated.reshape(local_sub, code_count, sub_dim))


def solution(mesh):
    placed = (
        P(("dom", "sub"), None),
        P(("dom", "sub")),
        P(("dom", "sub"), None),
        P("dom", "sub"),
        P("dom"),
        P("sub", None, None),
        P("sub", None),
    )
    return jax.shard_map(
        per_device,
        mesh=mesh,
        in_specs=placed,
        out_specs=(P("dom", "sub"), P(("dom", "sub"), None), P("sub", None, None)),
        check_vma=False,
    )
```

```python
import jax
import jax.numpy as jnp
from jax import lax
from jax.sharding import PartitionSpec as P

ITERS = 4
ID_BASE = 64


def split_dot(table, values):
    high = lax.reduce_precision(values, exponent_bits=8, mantissa_bits=7)
    low = (values - high).astype(jnp.bfloat16)
    width = values.shape[1]
    parts = jnp.concatenate([high.astype(jnp.bfloat16), low], axis=1)
    both = jnp.dot(table, parts, preferred_element_type=jnp.float32)
    return both[:, :width] + both[:, width:]


def exact_pick(pick_hi, pick_lo, table):
    high = lax.reduce_precision(table, exponent_bits=8, mantissa_bits=7)
    rest = table - high
    middle = lax.reduce_precision(rest, exponent_bits=8, mantissa_bits=7)
    low = rest - middle
    lanes = table.shape[1]
    parts = jnp.concatenate([high, middle, low], axis=1).astype(jnp.bfloat16)
    picked = jnp.dot(pick_hi, parts, preferred_element_type=jnp.float32)
    chosen = [
        jnp.sum(jnp.where(pick_lo, picked[:, k * lanes : (k + 1) * lanes], 0.0), axis=1) for k in range(3)
    ]
    return (chosen[0] + chosen[1]) + chosen[2]


def shift_sum(values, axis):
    count = lax.axis_size(axis)
    total = values
    for shift in range(1, count):
        pairs = [(source, (source + shift) % count) for source in range(count)]
        total = total + lax.ppermute(values, axis, pairs)
    return total


def ordered_sum(values, axis):
    count = lax.axis_size(axis)
    arrived = [values]
    for shift in range(1, count):
        pairs = [(source, (source + shift) % count) for source in range(count)]
        arrived.append(lax.ppermute(values, axis, pairs))
    stacked = jnp.stack(arrived)
    order = (lax.axis_index(axis) - jnp.arange(count, dtype=jnp.int32)) % count
    return jnp.sum(jnp.take(stacked, order, axis=0), axis=0)


def per_device(vectors, assign, codes, centroids, perp_ratio, codebook, codeword_weight_total):
    owners = lax.axis_size("dom")
    sub_count = lax.axis_size("sub")
    rows_dev, row_width = vectors.shape
    part_local, columns = centroids.shape
    local_sub, code_count, sub_dim = codebook.shape
    capacity = 2 * rows_dev // owners

    owner_of = assign // part_local
    owner_mask = owner_of[:, None] == jnp.arange(owners, dtype=jnp.int32)[None, :]
    counts = jnp.sum(owner_mask.astype(jnp.int32), axis=0)
    starts = jnp.cumsum(counts) - counts
    first_row_index = jnp.sum(jnp.where(owner_mask, starts[None, :], 0), axis=1)
    position = jnp.arange(rows_dev, dtype=jnp.int32) - first_row_index
    slot_index = owner_of * capacity + position
    source_rows = starts[:, None] + jnp.arange(capacity, dtype=jnp.int32)[None, :]
    usable_slot = jnp.arange(capacity, dtype=jnp.int32)[None, :] < counts[:, None]
    clipped = jnp.minimum(source_rows, rows_dev - 1)
    send_rows = jnp.where(
        usable_slot[:, :, None], jnp.take(vectors, clipped, axis=0), jnp.zeros((), jnp.bfloat16)
    )
    send_codes = jnp.take(codes, clipped, axis=0).astype(jnp.bfloat16)
    owner_base = (jnp.arange(owners, dtype=jnp.int32) * part_local)[:, None]
    send_ids = jnp.where(usable_slot, jnp.take(assign, clipped, axis=0) - owner_base, part_local)
    split_rows = send_rows.reshape(owners, capacity, sub_count, columns).transpose(0, 2, 1, 3)
    split_rows = split_rows.reshape(owners * sub_count, capacity, columns)
    split_codes = send_codes.reshape(owners, capacity, sub_count, local_sub).transpose(0, 2, 1, 3)
    split_codes = split_codes.reshape(owners * sub_count, capacity * local_sub // 128, 128)
    id_copies = jnp.broadcast_to(send_ids[:, None, :], (owners, sub_count, capacity))
    id_copies = id_copies.reshape(owners * sub_count, 1, capacity)
    slot_ids = lax.all_to_all(id_copies, ("dom", "sub"), split_axis=0, concat_axis=0, tiled=True)
    rows = lax.all_to_all(split_rows, ("dom", "sub"), split_axis=0, concat_axis=0, tiled=True)
    row_codes = lax.all_to_all(split_codes, ("dom", "sub"), split_axis=0, concat_axis=0, tiled=True)
    slot_ids = slot_ids.reshape(-1)
    rows = rows.reshape(-1, columns)
    row_codes = row_codes.reshape(-1, local_sub).astype(jnp.int32)
    usable = slot_ids < part_local
    safe_ids = jnp.minimum(slot_ids, part_local - 1)

    same = (slot_ids[:, None] == slot_ids[None, :]) & usable[:, None]
    same_table = same.astype(jnp.bfloat16)
    filled = jnp.sum(same.astype(jnp.float32), axis=1)
    floors = jnp.maximum(filled, 1.0)[:, None]
    sum_x = jnp.dot(same_table, rows, preferred_element_type=jnp.float32)
    as_float = rows.astype(jnp.float32)
    current = jnp.take(centroids, safe_ids, axis=0)
    digit_hi = slot_ids // ID_BASE
    digit_lo = slot_ids % ID_BASE
    block_count = part_local // ID_BASE
    pick_hi = (digit_hi[:, None] == jnp.arange(block_count, dtype=jnp.int32)[None, :]).astype(jnp.bfloat16)
    pick_lo = digit_lo[:, None] == jnp.arange(ID_BASE, dtype=jnp.int32)[None, :]
    weight_fractions = exact_pick(pick_hi, pick_lo, perp_ratio.reshape(block_count, ID_BASE))[:, None]
    filled_fraction = weight_fractions * filled[:, None]
    stats = shift_sum(
        jnp.stack([jnp.sum(as_float * as_float, axis=1), jnp.sum(as_float * current, axis=1)]), "sub"
    )
    norms = stats[0]
    inner = stats[1]
    for iteration in range(ITERS):
        if iteration > 0:
            inner = shift_sum(jnp.sum(as_float * current, axis=1), "sub")
        weight = inner / (norms + 1e-06)
        projected = split_dot(same_table, as_float * weight[:, None])
        current = (
            current
            - (filled_fraction * current + (1.0 - weight_fractions) * projected - sum_x) / floors
        )
    write_ids = jnp.where(usable, slot_ids, part_local)
    target = centroids + (slot_ids[0] * 0).astype(jnp.float32)
    new_centroids = target.at[write_ids].set(current, mode="drop")
    residual = jnp.where(usable[:, None], as_float - current, 0.0).astype(jnp.bfloat16)

    code_member = (
        (row_codes[:, :, None] == jnp.arange(code_count, dtype=jnp.int32)[None, None, :])
        & usable[:, None, None]
    ).astype(jnp.bfloat16)
    pieces = residual.reshape(-1, local_sub, sub_dim)
    book_sums = jnp.einsum("rmk,rmd->mkd", code_member, pieces, preferred_element_type=jnp.float32)
    book_counts = jnp.sum(code_member, axis=0, dtype=jnp.float32)
    packed = jnp.concatenate([book_sums.reshape(-1), book_counts.reshape(-1)])
    packed = ordered_sum(packed.reshape(-1, 128), "dom").reshape(-1)
    entries = local_sub * code_count
    totals = packed[: entries * sub_dim].reshape(entries, sub_dim)
    tallies = packed[entries * sub_dim :]
    weights = codeword_weight_total.reshape(entries, 1)
    updated = (codebook.reshape(entries, sub_dim) * weights + totals) / (weights + tallies[:, None])

    outgoing = residual.reshape(owners * sub_count, capacity, columns)
    returned = lax.all_to_all(outgoing, ("dom", "sub"), split_axis=0, concat_axis=0, tiled=True)
    returned = returned.reshape(owners, sub_count, capacity, columns).transpose(0, 2, 1, 3)
    flat_rows = returned.reshape(owners * capacity, row_width)
    residual_rows = jnp.take(flat_rows, slot_index, axis=0)
    return (new_centroids, residual_rows, updated.reshape(local_sub, code_count, sub_dim))


def solution(mesh):
    placed = (
        P(("dom", "sub"), None),
        P(("dom", "sub")),
        P(("dom", "sub"), None),
        P("dom", "sub"),
        P("dom"),
        P("sub", None, None),
        P("sub", None),
    )
    return jax.shard_map(
        per_device,
        mesh=mesh,
        in_specs=placed,
        out_specs=(P("dom", "sub"), P(("dom", "sub"), None), P("sub", None, None)),
        check_vma=False,
    )
```

```python
import jax
import jax.numpy as jnp
from jax import lax
from jax.sharding import PartitionSpec as P

ITERS = 4
ID_BASE = 64


def split_dot(table, values):
    high = lax.reduce_precision(values, exponent_bits=8, mantissa_bits=7)
    low = (values - high).astype(jnp.bfloat16)
    width = values.shape[1]
    parts = jnp.concatenate([high.astype(jnp.bfloat16), low], axis=1)
    both = jnp.dot(table, parts, preferred_element_type=jnp.float32)
    return both[:, :width] + both[:, width:]


def exact_pick(pick_hi, pick_lo, table):
    high = lax.reduce_precision(table, exponent_bits=8, mantissa_bits=7)
    rest = table - high
    middle = lax.reduce_precision(rest, exponent_bits=8, mantissa_bits=7)
    low = rest - middle
    lanes = table.shape[1]
    parts = jnp.concatenate([high, middle, low], axis=1).astype(jnp.bfloat16)
    picked = jnp.dot(pick_hi, parts, preferred_element_type=jnp.float32)
    chosen = [
        jnp.sum(jnp.where(pick_lo, picked[:, k * lanes : (k + 1) * lanes], 0.0), axis=1) for k in range(3)
    ]
    return (chosen[0] + chosen[1]) + chosen[2]


def shift_sum(values, axis):
    count = lax.axis_size(axis)
    total = values
    for shift in range(1, count):
        pairs = [(source, (source + shift) % count) for source in range(count)]
        total = total + lax.ppermute(values, axis, pairs)
    return total


def ordered_sum(values, axis):
    count = lax.axis_size(axis)
    arrived = [values]
    for shift in range(1, count):
        pairs = [(source, (source + shift) % count) for source in range(count)]
        arrived.append(lax.ppermute(values, axis, pairs))
    stacked = jnp.stack(arrived)
    order = (lax.axis_index(axis) - jnp.arange(count, dtype=jnp.int32)) % count
    return jnp.sum(jnp.take(stacked, order, axis=0), axis=0)


def per_device(vectors, assign, codes, centroids, perp_ratio, codebook, codeword_weight_total):
    owners = lax.axis_size("dom")
    sub_count = lax.axis_size("sub")
    rows_dev, row_width = vectors.shape
    part_local, columns = centroids.shape
    local_sub, code_count, sub_dim = codebook.shape
    capacity = 2 * rows_dev // owners

    owner_of = assign // part_local
    owner_mask = owner_of[:, None] == jnp.arange(owners, dtype=jnp.int32)[None, :]
    counts = jnp.sum(owner_mask.astype(jnp.int32), axis=0)
    starts = jnp.cumsum(counts) - counts
    first_row_index = jnp.sum(jnp.where(owner_mask, starts[None, :], 0), axis=1)
    position = jnp.arange(rows_dev, dtype=jnp.int32) - first_row_index
    slot_index = owner_of * capacity + position
    source_rows = starts[:, None] + jnp.arange(capacity, dtype=jnp.int32)[None, :]
    usable_slot = jnp.arange(capacity, dtype=jnp.int32)[None, :] < counts[:, None]
    clipped = jnp.minimum(source_rows, rows_dev - 1)
    send_rows = jnp.where(
        usable_slot[:, :, None], jnp.take(vectors, clipped, axis=0), jnp.zeros((), jnp.bfloat16)
    )
    send_codes = jnp.take(codes, clipped, axis=0).astype(jnp.bfloat16)
    owner_base = (jnp.arange(owners, dtype=jnp.int32) * part_local)[:, None]
    send_ids = jnp.where(usable_slot, jnp.take(assign, clipped, axis=0) - owner_base, part_local)
    split_rows = send_rows.reshape(owners, capacity, sub_count, columns).transpose(0, 2, 1, 3)
    split_rows = split_rows.reshape(owners * sub_count, capacity, columns)
    split_codes = send_codes.reshape(owners, capacity, sub_count, local_sub).transpose(0, 2, 1, 3)
    split_codes = split_codes.reshape(owners * sub_count, capacity * local_sub // 128, 128)
    id_copies = jnp.broadcast_to(send_ids[:, None, :], (owners, sub_count, capacity))
    id_copies = id_copies.reshape(owners * sub_count, 1, capacity)
    slot_ids = lax.all_to_all(id_copies, ("dom", "sub"), split_axis=0, concat_axis=0, tiled=True)
    rows = lax.all_to_all(split_rows, ("dom", "sub"), split_axis=0, concat_axis=0, tiled=True)
    row_codes = lax.all_to_all(split_codes, ("dom", "sub"), split_axis=0, concat_axis=0, tiled=True)
    slot_ids = slot_ids.reshape(-1)
    rows = rows.reshape(-1, columns)
    row_codes = row_codes.reshape(-1, local_sub).astype(jnp.int32)
    usable = slot_ids < part_local
    safe_ids = jnp.minimum(slot_ids, part_local - 1)

    same = (slot_ids[:, None] == slot_ids[None, :]) & usable[:, None]
    same_table = same.astype(jnp.bfloat16)
    filled = jnp.sum(same.astype(jnp.float32), axis=1)
    floors = jnp.maximum(filled, 1.0)[:, None]
    sum_x = jnp.dot(same_table, rows, preferred_element_type=jnp.float32)
    as_float = rows.astype(jnp.float32)
    current = jnp.take(centroids, safe_ids, axis=0)
    digit_hi = slot_ids // ID_BASE
    digit_lo = slot_ids % ID_BASE
    block_count = part_local // ID_BASE
    pick_hi = (digit_hi[:, None] == jnp.arange(block_count, dtype=jnp.int32)[None, :]).astype(jnp.bfloat16)
    pick_lo = digit_lo[:, None] == jnp.arange(ID_BASE, dtype=jnp.int32)[None, :]
    weight_fractions = exact_pick(pick_hi, pick_lo, perp_ratio.reshape(block_count, ID_BASE))[:, None]
    filled_fraction = weight_fractions * filled[:, None]
    stats = shift_sum(
        jnp.stack([jnp.sum(as_float * as_float, axis=1), jnp.sum(as_float * current, axis=1)]), "sub"
    )
    norms = stats[0]
    inner = stats[1]
    for iteration in range(ITERS):
        if iteration > 0:
            inner = shift_sum(jnp.sum(as_float * current, axis=1), "sub")
        weight = inner / (norms + 1e-06)
        projected = split_dot(same_table, as_float * weight[:, None])
        current = (
            current
            - (filled_fraction * current + (1.0 - weight_fractions) * projected - sum_x) / floors
        )
    write_ids = jnp.where(usable, slot_ids, part_local)
    target = centroids + slot_ids[0].astype(jnp.float32) * 0.0
    new_centroids = target.at[write_ids].set(current, mode="drop")
    residual = jnp.where(usable[:, None], as_float - current, 0.0).astype(jnp.bfloat16)

    code_member = (
        (row_codes[:, :, None] == jnp.arange(code_count, dtype=jnp.int32)[None, None, :])
        & usable[:, None, None]
    ).astype(jnp.bfloat16)
    pieces = residual.reshape(-1, local_sub, sub_dim)
    book_sums = jnp.einsum("rmk,rmd->mkd", code_member, pieces, preferred_element_type=jnp.float32)
    book_counts = jnp.sum(code_member, axis=0, dtype=jnp.float32)
    packed = jnp.concatenate([book_sums.reshape(-1), book_counts.reshape(-1)])
    packed = ordered_sum(packed.reshape(-1, 128), "dom").reshape(-1)
    entries = local_sub * code_count
    totals = packed[: entries * sub_dim].reshape(entries, sub_dim)
    tallies = packed[entries * sub_dim :]
    weights = codeword_weight_total.reshape(entries, 1)
    updated = (codebook.reshape(entries, sub_dim) * weights + totals) / (weights + tallies[:, None])

    outgoing = residual.reshape(owners * sub_count, capacity, columns)
    returned = lax.all_to_all(outgoing, ("dom", "sub"), split_axis=0, concat_axis=0, tiled=True)
    returned = returned.reshape(owners, sub_count, capacity, columns).transpose(0, 2, 1, 3)
    flat_rows = returned.reshape(owners * capacity, row_width)
    residual_rows = jnp.take(flat_rows, slot_index, axis=0)
    return (new_centroids, residual_rows, updated.reshape(local_sub, code_count, sub_dim))


def solution(mesh):
    placed = (
        P(("dom", "sub"), None),
        P(("dom", "sub")),
        P(("dom", "sub"), None),
        P("dom", "sub"),
        P("dom"),
        P("sub", None, None),
        P("sub", None),
    )
    return jax.shard_map(
        per_device,
        mesh=mesh,
        in_specs=placed,
        out_specs=(P("dom", "sub"), P(("dom", "sub"), None), P("sub", None, None)),
        check_vma=False,
    )
```

```python
import jax
import jax.numpy as jnp
from jax import lax
from jax.sharding import PartitionSpec as P

ITERS = 4
ID_BASE = 64


def split_dot(table, values):
    high = lax.reduce_precision(values, exponent_bits=8, mantissa_bits=7)
    low = (values - high).astype(jnp.bfloat16)
    width = values.shape[1]
    parts = jnp.concatenate([high.astype(jnp.bfloat16), low], axis=1)
    both = jnp.dot(table, parts, preferred_element_type=jnp.float32)
    return both[:, :width] + both[:, width:]


def exact_pick(pick_hi, pick_lo, table):
    high = lax.reduce_precision(table, exponent_bits=8, mantissa_bits=7)
    rest = table - high
    middle = lax.reduce_precision(rest, exponent_bits=8, mantissa_bits=7)
    low = rest - middle
    lanes = table.shape[1]
    parts = jnp.concatenate([high, middle, low], axis=1).astype(jnp.bfloat16)
    picked = jnp.dot(pick_hi, parts, preferred_element_type=jnp.float32)
    chosen = [
        jnp.sum(jnp.where(pick_lo, picked[:, k * lanes : (k + 1) * lanes], 0.0), axis=1) for k in range(3)
    ]
    return (chosen[0] + chosen[1]) + chosen[2]


def shift_sum(values, axis):
    count = lax.axis_size(axis)
    total = values
    for shift in range(1, count):
        pairs = [(source, (source + shift) % count) for source in range(count)]
        total = total + lax.ppermute(values, axis, pairs)
    return total


def ordered_sum(values, axis):
    count = lax.axis_size(axis)
    arrived = [values]
    for shift in range(1, count):
        pairs = [(source, (source + shift) % count) for source in range(count)]
        arrived.append(lax.ppermute(values, axis, pairs))
    stacked = jnp.stack(arrived)
    order = (lax.axis_index(axis) - jnp.arange(count, dtype=jnp.int32)) % count
    return jnp.sum(jnp.take(stacked, order, axis=0), axis=0)


def per_device(vectors, assign, codes, centroids, perp_ratio, codebook, codeword_weight_total):
    owners = lax.axis_size("dom")
    sub_count = lax.axis_size("sub")
    rows_dev, row_width = vectors.shape
    part_local, columns = centroids.shape
    local_sub, code_count, sub_dim = codebook.shape
    capacity = 2 * rows_dev // owners

    owner_of = assign // part_local
    owner_mask = owner_of[:, None] == jnp.arange(owners, dtype=jnp.int32)[None, :]
    counts = jnp.sum(owner_mask.astype(jnp.int32), axis=0)
    starts = jnp.cumsum(counts) - counts
    first_row_index = jnp.sum(jnp.where(owner_mask, starts[None, :], 0), axis=1)
    position = jnp.arange(rows_dev, dtype=jnp.int32) - first_row_index
    slot_index = owner_of * capacity + position
    source_rows = starts[:, None] + jnp.arange(capacity, dtype=jnp.int32)[None, :]
    usable_slot = jnp.arange(capacity, dtype=jnp.int32)[None, :] < counts[:, None]
    clipped = jnp.minimum(source_rows, rows_dev - 1)
    send_rows = jnp.where(
        usable_slot[:, :, None], jnp.take(vectors, clipped, axis=0), jnp.zeros((), jnp.bfloat16)
    )
    send_codes = jnp.take(codes, clipped, axis=0).astype(jnp.bfloat16)
    owner_base = (jnp.arange(owners, dtype=jnp.int32) * part_local)[:, None]
    send_ids = jnp.where(usable_slot, jnp.take(assign, clipped, axis=0) - owner_base, part_local)
    split_rows = send_rows.reshape(owners, capacity, sub_count, columns).transpose(0, 2, 1, 3)
    split_rows = split_rows.reshape(owners * sub_count, capacity, columns)
    id_parts = jnp.stack([send_ids // ID_BASE, send_ids % ID_BASE], axis=-1).astype(jnp.bfloat16)
    meta = jnp.concatenate(
        [
            jnp.broadcast_to(id_parts[:, None, :, :], (owners, sub_count, capacity, 2)).reshape(
                owners, sub_count, capacity * 2
            ),
            send_codes.reshape(owners, capacity, sub_count, local_sub)
            .transpose(0, 2, 1, 3)
            .reshape(owners, sub_count, capacity * local_sub),
        ],
        axis=-1,
    )
    meta_rows = -(-(capacity * (local_sub + 2)) // 128)
    meta = meta.reshape(owners * sub_count, capacity * (local_sub + 2))
    meta = jnp.pad(meta, ((0, 0), (0, meta_rows * 128 - capacity * (local_sub + 2))))
    meta = meta.reshape(owners * sub_count, meta_rows, 128)
    meta = lax.all_to_all(meta, ("dom", "sub"), split_axis=0, concat_axis=0, tiled=True)
    rows = lax.all_to_all(split_rows, ("dom", "sub"), split_axis=0, concat_axis=0, tiled=True)
    meta = meta.reshape(owners * sub_count, meta_rows * 128)
    id_floats = meta[:, : capacity * 2].reshape(-1, 2).astype(jnp.float32)
    slot_ids = (id_floats[:, 0] * ID_BASE + id_floats[:, 1]).astype(jnp.int32)
    row_codes = meta[:, capacity * 2 : capacity * (local_sub + 2)].reshape(-1, local_sub).astype(jnp.int32)
    rows = rows.reshape(-1, columns)
    usable = slot_ids < part_local
    safe_ids = jnp.minimum(slot_ids, part_local - 1)

    same = (slot_ids[:, None] == slot_ids[None, :]) & usable[:, None]
    same_table = same.astype(jnp.bfloat16)
    filled = jnp.sum(same.astype(jnp.float32), axis=1)
    floors = jnp.maximum(filled, 1.0)[:, None]
    sum_x = jnp.dot(same_table, rows, preferred_element_type=jnp.float32)
    as_float = rows.astype(jnp.float32)
    current = jnp.take(centroids, safe_ids, axis=0)
    digit_hi = slot_ids // ID_BASE
    digit_lo = slot_ids % ID_BASE
    block_count = part_local // ID_BASE
    pick_hi = (digit_hi[:, None] == jnp.arange(block_count, dtype=jnp.int32)[None, :]).astype(jnp.bfloat16)
    pick_lo = digit_lo[:, None] == jnp.arange(ID_BASE, dtype=jnp.int32)[None, :]
    weight_fractions = exact_pick(pick_hi, pick_lo, perp_ratio.reshape(block_count, ID_BASE))[:, None]
    filled_fraction = weight_fractions * filled[:, None]
    stats = shift_sum(
        jnp.stack([jnp.sum(as_float * as_float, axis=1), jnp.sum(as_float * current, axis=1)]), "sub"
    )
    norms = stats[0]
    inner = stats[1]
    for iteration in range(ITERS):
        if iteration > 0:
            inner = shift_sum(jnp.sum(as_float * current, axis=1), "sub")
        weight = inner / (norms + 1e-06)
        projected = split_dot(same_table, as_float * weight[:, None])
        current = (
            current
            - (filled_fraction * current + (1.0 - weight_fractions) * projected - sum_x) / floors
        )
    write_ids = jnp.where(usable, slot_ids, part_local)
    target = centroids + slot_ids[0].astype(jnp.float32) * 0.0
    new_centroids = target.at[write_ids].set(current, mode="drop")
    residual = jnp.where(usable[:, None], as_float - current, 0.0).astype(jnp.bfloat16)

    code_member = (
        (row_codes[:, :, None] == jnp.arange(code_count, dtype=jnp.int32)[None, None, :])
        & usable[:, None, None]
    ).astype(jnp.bfloat16)
    pieces = residual.reshape(-1, local_sub, sub_dim)
    book_sums = jnp.einsum("rmk,rmd->mkd", code_member, pieces, preferred_element_type=jnp.float32)
    book_counts = jnp.sum(code_member, axis=0, dtype=jnp.float32)
    packed = jnp.concatenate([book_sums.reshape(-1), book_counts.reshape(-1)])
    packed = ordered_sum(packed.reshape(-1, 128), "dom").reshape(-1)
    entries = local_sub * code_count
    totals = packed[: entries * sub_dim].reshape(entries, sub_dim)
    tallies = packed[entries * sub_dim :]
    weights = codeword_weight_total.reshape(entries, 1)
    updated = (codebook.reshape(entries, sub_dim) * weights + totals) / (weights + tallies[:, None])

    outgoing = residual.reshape(owners * sub_count, capacity, columns)
    returned = lax.all_to_all(outgoing, ("dom", "sub"), split_axis=0, concat_axis=0, tiled=True)
    returned = returned.reshape(owners, sub_count, capacity, columns).transpose(0, 2, 1, 3)
    flat_rows = returned.reshape(owners * capacity, row_width)
    residual_rows = jnp.take(flat_rows, slot_index, axis=0)
    return (new_centroids, residual_rows, updated.reshape(local_sub, code_count, sub_dim))


def solution(mesh):
    placed = (
        P(("dom", "sub"), None),
        P(("dom", "sub")),
        P(("dom", "sub"), None),
        P("dom", "sub"),
        P("dom"),
        P("sub", None, None),
        P("sub", None),
    )
    return jax.shard_map(
        per_device,
        mesh=mesh,
        in_specs=placed,
        out_specs=(P("dom", "sub"), P(("dom", "sub"), None), P("sub", None, None)),
        check_vma=False,
    )
```

```python
import jax
import jax.numpy as jnp
from jax import lax
from jax.sharding import PartitionSpec as P

ITERS = 4
ID_BASE = 64


def split_dot(table, values):
    high = lax.reduce_precision(values, exponent_bits=8, mantissa_bits=7)
    low = (values - high).astype(jnp.bfloat16)
    width = values.shape[1]
    parts = jnp.concatenate([high.astype(jnp.bfloat16), low], axis=1)
    both = jnp.dot(table, parts, preferred_element_type=jnp.float32)
    return both[:, :width] + both[:, width:]


def exact_pick(pick_hi, pick_lo, table):
    high = lax.reduce_precision(table, exponent_bits=8, mantissa_bits=7)
    rest = table - high
    middle = lax.reduce_precision(rest, exponent_bits=8, mantissa_bits=7)
    low = rest - middle
    lanes = table.shape[1]
    parts = jnp.concatenate([high, middle, low], axis=1).astype(jnp.bfloat16)
    picked = jnp.dot(pick_hi, parts, preferred_element_type=jnp.float32)
    chosen = [
        jnp.sum(jnp.where(pick_lo, picked[:, k * lanes : (k + 1) * lanes], 0.0), axis=1) for k in range(3)
    ]
    return (chosen[0] + chosen[1]) + chosen[2]


def shift_sum(values, axis):
    count = lax.axis_size(axis)
    total = values
    for shift in range(1, count):
        pairs = [(source, (source + shift) % count) for source in range(count)]
        total = total + lax.ppermute(values, axis, pairs)
    return total


def ordered_sum(values, axis):
    count = lax.axis_size(axis)
    arrived = [values]
    for shift in range(1, count):
        pairs = [(source, (source + shift) % count) for source in range(count)]
        arrived.append(lax.ppermute(values, axis, pairs))
    stacked = jnp.stack(arrived)
    order = (lax.axis_index(axis) - jnp.arange(count, dtype=jnp.int32)) % count
    return jnp.sum(jnp.take(stacked, order, axis=0), axis=0)


def per_device(vectors, assign, codes, centroids, perp_ratio, codebook, codeword_weight_total):
    owners = lax.axis_size("dom")
    sub_count = lax.axis_size("sub")
    rows_dev, row_width = vectors.shape
    part_local, columns = centroids.shape
    local_sub, code_count, sub_dim = codebook.shape
    capacity = 2 * rows_dev // owners

    owner_of = assign // part_local
    owner_mask = owner_of[:, None] == jnp.arange(owners, dtype=jnp.int32)[None, :]
    counts = jnp.sum(owner_mask.astype(jnp.int32), axis=0)
    starts = jnp.cumsum(counts) - counts
    first_row_index = jnp.sum(jnp.where(owner_mask, starts[None, :], 0), axis=1)
    position = jnp.arange(rows_dev, dtype=jnp.int32) - first_row_index
    slot_index = owner_of * capacity + position
    source_rows = starts[:, None] + jnp.arange(capacity, dtype=jnp.int32)[None, :]
    usable_slot = jnp.arange(capacity, dtype=jnp.int32)[None, :] < counts[:, None]
    clipped = jnp.minimum(source_rows, rows_dev - 1)
    send_rows = jnp.where(
        usable_slot[:, :, None], jnp.take(vectors, clipped, axis=0), jnp.zeros((), jnp.bfloat16)
    )
    owner_base = (jnp.arange(owners, dtype=jnp.int32) * part_local)[:, None]
    send_ids = jnp.where(usable_slot, jnp.take(assign, clipped, axis=0) - owner_base, part_local)
    split_rows = send_rows.reshape(owners, capacity, sub_count, columns).transpose(0, 2, 1, 3)
    split_rows = split_rows.reshape(owners * sub_count, capacity, columns)
    id_copies = jnp.broadcast_to(send_ids[:, None, :], (owners, sub_count, capacity))
    id_copies = id_copies.reshape(owners * sub_count, 1, capacity)
    slot_ids = lax.all_to_all(id_copies, ("dom", "sub"), split_axis=0, concat_axis=0, tiled=True)
    rows = lax.all_to_all(split_rows, ("dom", "sub"), split_axis=0, concat_axis=0, tiled=True)
    late_zero = rows[0, 0, 0] * 0
    send_codes = jnp.take(codes, clipped, axis=0).astype(jnp.bfloat16) + late_zero
    split_codes = send_codes.reshape(owners, capacity, sub_count, local_sub).transpose(0, 2, 1, 3)
    split_codes = split_codes.reshape(owners * sub_count, capacity * local_sub // 128, 128)
    row_codes = lax.all_to_all(split_codes, ("dom", "sub"), split_axis=0, concat_axis=0, tiled=True)
    slot_ids = slot_ids.reshape(-1)
    rows = rows.reshape(-1, columns)
    row_codes = row_codes.reshape(-1, local_sub).astype(jnp.int32)
    usable = slot_ids < part_local
    safe_ids = jnp.minimum(slot_ids, part_local - 1)

    same = (slot_ids[:, None] == slot_ids[None, :]) & usable[:, None]
    same_table = same.astype(jnp.bfloat16)
    filled = jnp.sum(same.astype(jnp.float32), axis=1)
    floors = jnp.maximum(filled, 1.0)[:, None]
    sum_x = jnp.dot(same_table, rows, preferred_element_type=jnp.float32)
    as_float = rows.astype(jnp.float32)
    current = jnp.take(centroids, safe_ids, axis=0)
    digit_hi = slot_ids // ID_BASE
    digit_lo = slot_ids % ID_BASE
    block_count = part_local // ID_BASE
    pick_hi = (digit_hi[:, None] == jnp.arange(block_count, dtype=jnp.int32)[None, :]).astype(jnp.bfloat16)
    pick_lo = digit_lo[:, None] == jnp.arange(ID_BASE, dtype=jnp.int32)[None, :]
    weight_fractions = exact_pick(pick_hi, pick_lo, perp_ratio.reshape(block_count, ID_BASE))[:, None]
    filled_fraction = weight_fractions * filled[:, None]
    stats = shift_sum(
        jnp.stack([jnp.sum(as_float * as_float, axis=1), jnp.sum(as_float * current, axis=1)]), "sub"
    )
    norms = stats[0]
    inner = stats[1]
    for iteration in range(ITERS):
        if iteration > 0:
            inner = shift_sum(jnp.sum(as_float * current, axis=1), "sub")
        weight = inner / (norms + 1e-06)
        projected = split_dot(same_table, as_float * weight[:, None])
        current = (
            current
            - (filled_fraction * current + (1.0 - weight_fractions) * projected - sum_x) / floors
        )
    write_ids = jnp.where(usable, slot_ids, part_local)
    target = centroids + slot_ids[0].astype(jnp.float32) * 0.0
    new_centroids = target.at[write_ids].set(current, mode="drop")
    residual = jnp.where(usable[:, None], as_float - current, 0.0).astype(jnp.bfloat16)

    code_member = (
        (row_codes[:, :, None] == jnp.arange(code_count, dtype=jnp.int32)[None, None, :])
        & usable[:, None, None]
    ).astype(jnp.bfloat16)
    pieces = residual.reshape(-1, local_sub, sub_dim)
    book_sums = jnp.einsum("rmk,rmd->mkd", code_member, pieces, preferred_element_type=jnp.float32)
    book_counts = jnp.sum(code_member, axis=0, dtype=jnp.float32)
    packed = jnp.concatenate([book_sums.reshape(-1), book_counts.reshape(-1)])
    packed = ordered_sum(packed.reshape(-1, 128), "dom").reshape(-1)
    entries = local_sub * code_count
    totals = packed[: entries * sub_dim].reshape(entries, sub_dim)
    tallies = packed[entries * sub_dim :]
    weights = codeword_weight_total.reshape(entries, 1)
    updated = (codebook.reshape(entries, sub_dim) * weights + totals) / (weights + tallies[:, None])

    outgoing = residual.reshape(owners * sub_count, capacity, columns)
    returned = lax.all_to_all(outgoing, ("dom", "sub"), split_axis=0, concat_axis=0, tiled=True)
    returned = returned.reshape(owners, sub_count, capacity, columns).transpose(0, 2, 1, 3)
    flat_rows = returned.reshape(owners * capacity, row_width)
    residual_rows = jnp.take(flat_rows, slot_index, axis=0)
    return (new_centroids, residual_rows, updated.reshape(local_sub, code_count, sub_dim))


def solution(mesh):
    placed = (
        P(("dom", "sub"), None),
        P(("dom", "sub")),
        P(("dom", "sub"), None),
        P("dom", "sub"),
        P("dom"),
        P("sub", None, None),
        P("sub", None),
    )
    return jax.shard_map(
        per_device,
        mesh=mesh,
        in_specs=placed,
        out_specs=(P("dom", "sub"), P(("dom", "sub"), None), P("sub", None, None)),
        check_vma=False,
    )
```

```python
import jax
import jax.numpy as jnp
from jax import lax
from jax.sharding import PartitionSpec as P

ITERS = 4
ID_BASE = 64


def split_dot(table, values):
    high = lax.reduce_precision(values, exponent_bits=8, mantissa_bits=7)
    low = (values - high).astype(jnp.bfloat16)
    width = values.shape[1]
    parts = jnp.concatenate([high.astype(jnp.bfloat16), low], axis=1)
    both = jnp.dot(table, parts, preferred_element_type=jnp.float32)
    return both[:, :width] + both[:, width:]


def exact_pick(pick_hi, pick_lo, table):
    high = lax.reduce_precision(table, exponent_bits=8, mantissa_bits=7)
    rest = table - high
    middle = lax.reduce_precision(rest, exponent_bits=8, mantissa_bits=7)
    low = rest - middle
    lanes = table.shape[1]
    parts = jnp.concatenate([high, middle, low], axis=1).astype(jnp.bfloat16)
    picked = jnp.dot(pick_hi, parts, preferred_element_type=jnp.float32)
    chosen = [
        jnp.sum(jnp.where(pick_lo, picked[:, k * lanes : (k + 1) * lanes], 0.0), axis=1) for k in range(3)
    ]
    return (chosen[0] + chosen[1]) + chosen[2]


def shift_sum(values, axis):
    count = lax.axis_size(axis)
    total = values
    for shift in range(1, count):
        pairs = [(source, (source + shift) % count) for source in range(count)]
        total = total + lax.ppermute(values, axis, pairs)
    return total


def ordered_sum(values, axis):
    count = lax.axis_size(axis)
    arrived = [values]
    for shift in range(1, count):
        pairs = [(source, (source + shift) % count) for source in range(count)]
        arrived.append(lax.ppermute(values, axis, pairs))
    stacked = jnp.stack(arrived)
    order = (lax.axis_index(axis) - jnp.arange(count, dtype=jnp.int32)) % count
    return jnp.sum(jnp.take(stacked, order, axis=0, mode="clip"), axis=0)


def per_device(vectors, assign, codes, centroids, perp_ratio, codebook, codeword_weight_total):
    owners = lax.axis_size("dom")
    sub_count = lax.axis_size("sub")
    rows_dev, row_width = vectors.shape
    part_local, columns = centroids.shape
    local_sub, code_count, sub_dim = codebook.shape
    capacity = 2 * rows_dev // owners

    owner_of = assign // part_local
    owner_mask = owner_of[:, None] == jnp.arange(owners, dtype=jnp.int32)[None, :]
    counts = jnp.sum(owner_mask.astype(jnp.int32), axis=0)
    starts = jnp.cumsum(counts) - counts
    first_row_index = jnp.sum(jnp.where(owner_mask, starts[None, :], 0), axis=1)
    position = jnp.arange(rows_dev, dtype=jnp.int32) - first_row_index
    slot_index = owner_of * capacity + position
    source_rows = starts[:, None] + jnp.arange(capacity, dtype=jnp.int32)[None, :]
    usable_slot = jnp.arange(capacity, dtype=jnp.int32)[None, :] < counts[:, None]
    clipped = jnp.minimum(source_rows, rows_dev - 1)
    send_rows = jnp.where(
        usable_slot[:, :, None], jnp.take(vectors, clipped, axis=0, mode="clip"), jnp.zeros((), jnp.bfloat16)
    )
    send_codes = jnp.take(codes, clipped, axis=0, mode="clip").astype(jnp.bfloat16)
    owner_base = (jnp.arange(owners, dtype=jnp.int32) * part_local)[:, None]
    send_ids = jnp.where(usable_slot, jnp.take(assign, clipped, axis=0, mode="clip") - owner_base, part_local)
    split_rows = send_rows.reshape(owners, capacity, sub_count, columns).transpose(0, 2, 1, 3)
    split_rows = split_rows.reshape(owners * sub_count, capacity, columns)
    split_codes = send_codes.reshape(owners, capacity, sub_count, local_sub).transpose(0, 2, 1, 3)
    split_codes = split_codes.reshape(owners * sub_count, capacity * local_sub // 128, 128)
    id_copies = jnp.broadcast_to(send_ids[:, None, :], (owners, sub_count, capacity))
    id_copies = id_copies.reshape(owners * sub_count, 1, capacity)
    slot_ids = lax.all_to_all(id_copies, ("dom", "sub"), split_axis=0, concat_axis=0, tiled=True)
    rows = lax.all_to_all(split_rows, ("dom", "sub"), split_axis=0, concat_axis=0, tiled=True)
    row_codes = lax.all_to_all(split_codes, ("dom", "sub"), split_axis=0, concat_axis=0, tiled=True)
    slot_ids = slot_ids.reshape(-1)
    rows = rows.reshape(-1, columns)
    row_codes = row_codes.reshape(-1, local_sub).astype(jnp.int32)
    usable = slot_ids < part_local
    safe_ids = jnp.minimum(slot_ids, part_local - 1)

    same = (slot_ids[:, None] == slot_ids[None, :]) & usable[:, None]
    same_table = same.astype(jnp.bfloat16)
    filled = jnp.sum(same.astype(jnp.float32), axis=1)
    floors = jnp.maximum(filled, 1.0)[:, None]
    sum_x = jnp.dot(same_table, rows, preferred_element_type=jnp.float32)
    as_float = rows.astype(jnp.float32)
    current = jnp.take(centroids, safe_ids, axis=0, mode="clip")
    digit_hi = slot_ids // ID_BASE
    digit_lo = slot_ids % ID_BASE
    block_count = part_local // ID_BASE
    pick_hi = (digit_hi[:, None] == jnp.arange(block_count, dtype=jnp.int32)[None, :]).astype(jnp.bfloat16)
    pick_lo = digit_lo[:, None] == jnp.arange(ID_BASE, dtype=jnp.int32)[None, :]
    weight_fractions = exact_pick(pick_hi, pick_lo, perp_ratio.reshape(block_count, ID_BASE))[:, None]
    filled_fraction = weight_fractions * filled[:, None]
    stats = shift_sum(
        jnp.stack([jnp.sum(as_float * as_float, axis=1), jnp.sum(as_float * current, axis=1)]), "sub"
    )
    norms = stats[0]
    inner = stats[1]
    for iteration in range(ITERS):
        if iteration > 0:
            inner = shift_sum(jnp.sum(as_float * current, axis=1), "sub")
        weight = inner / (norms + 1e-06)
        projected = split_dot(same_table, as_float * weight[:, None])
        current = (
            current
            - (filled_fraction * current + (1.0 - weight_fractions) * projected - sum_x) / floors
        )
    write_ids = jnp.where(usable, slot_ids, part_local)
    target = centroids + slot_ids[0].astype(jnp.float32) * 0.0
    new_centroids = target.at[write_ids].set(current, mode="drop")
    residual = jnp.where(usable[:, None], as_float - current, 0.0).astype(jnp.bfloat16)

    code_member = (
        (row_codes[:, :, None] == jnp.arange(code_count, dtype=jnp.int32)[None, None, :])
        & usable[:, None, None]
    ).astype(jnp.bfloat16)
    pieces = residual.reshape(-1, local_sub, sub_dim)
    book_sums = jnp.einsum("rmk,rmd->mkd", code_member, pieces, preferred_element_type=jnp.float32)
    book_counts = jnp.sum(code_member, axis=0, dtype=jnp.float32)
    packed = jnp.concatenate([book_sums.reshape(-1), book_counts.reshape(-1)])
    packed = ordered_sum(packed.reshape(-1, 128), "dom").reshape(-1)
    entries = local_sub * code_count
    totals = packed[: entries * sub_dim].reshape(entries, sub_dim)
    tallies = packed[entries * sub_dim :]
    weights = codeword_weight_total.reshape(entries, 1)
    updated = (codebook.reshape(entries, sub_dim) * weights + totals) / (weights + tallies[:, None])

    outgoing = residual.reshape(owners * sub_count, capacity, columns)
    returned = lax.all_to_all(outgoing, ("dom", "sub"), split_axis=0, concat_axis=0, tiled=True)
    returned = returned.reshape(owners, sub_count, capacity, columns).transpose(0, 2, 1, 3)
    flat_rows = returned.reshape(owners * capacity, row_width)
    residual_rows = jnp.take(flat_rows, slot_index, axis=0, mode="clip")
    return (new_centroids, residual_rows, updated.reshape(local_sub, code_count, sub_dim))


def solution(mesh):
    placed = (
        P(("dom", "sub"), None),
        P(("dom", "sub")),
        P(("dom", "sub"), None),
        P("dom", "sub"),
        P("dom"),
        P("sub", None, None),
        P("sub", None),
    )
    return jax.shard_map(
        per_device,
        mesh=mesh,
        in_specs=placed,
        out_specs=(P("dom", "sub"), P(("dom", "sub"), None), P("sub", None, None)),
        check_vma=False,
    )
```

```python
import jax
import jax.numpy as jnp
from jax import lax
from jax.sharding import PartitionSpec as P

ITERS = 4
ID_BASE = 64


def split_dot(table, values):
    high = lax.reduce_precision(values, exponent_bits=8, mantissa_bits=7)
    low = (values - high).astype(jnp.bfloat16)
    width = values.shape[1]
    parts = jnp.concatenate([high.astype(jnp.bfloat16), low], axis=1)
    both = jnp.dot(table, parts, preferred_element_type=jnp.float32)
    return both[:, :width] + both[:, width:]


def exact_pick(pick_hi, pick_lo, table):
    high = lax.reduce_precision(table, exponent_bits=8, mantissa_bits=7)
    rest = table - high
    middle = lax.reduce_precision(rest, exponent_bits=8, mantissa_bits=7)
    low = rest - middle
    lanes = table.shape[1]
    parts = jnp.concatenate([high, middle, low], axis=1).astype(jnp.bfloat16)
    picked = jnp.dot(pick_hi, parts, preferred_element_type=jnp.float32)
    chosen = [
        jnp.sum(jnp.where(pick_lo, picked[:, k * lanes : (k + 1) * lanes], 0.0), axis=1) for k in range(3)
    ]
    return (chosen[0] + chosen[1]) + chosen[2]


def shift_sum(values, axis):
    count = lax.axis_size(axis)
    total = values
    for shift in range(1, count):
        pairs = [(source, (source + shift) % count) for source in range(count)]
        total = total + lax.ppermute(values, axis, pairs)
    return total


def butterfly_sum(values, axis):
    count = lax.axis_size(axis)
    total = values
    step = 1
    while step < count:
        pairs = [(source, source ^ step) for source in range(count)]
        total = total + lax.ppermute(total, axis, pairs)
        step *= 2
    return total


def per_device(vectors, assign, codes, centroids, perp_ratio, codebook, codeword_weight_total):
    owners = lax.axis_size("dom")
    sub_count = lax.axis_size("sub")
    rows_dev, row_width = vectors.shape
    part_local, columns = centroids.shape
    local_sub, code_count, sub_dim = codebook.shape
    capacity = 2 * rows_dev // owners

    owner_of = assign // part_local
    owner_mask = owner_of[:, None] == jnp.arange(owners, dtype=jnp.int32)[None, :]
    counts = jnp.sum(owner_mask.astype(jnp.int32), axis=0)
    starts = jnp.cumsum(counts) - counts
    first_row_index = jnp.sum(jnp.where(owner_mask, starts[None, :], 0), axis=1)
    position = jnp.arange(rows_dev, dtype=jnp.int32) - first_row_index
    slot_index = owner_of * capacity + position
    source_rows = starts[:, None] + jnp.arange(capacity, dtype=jnp.int32)[None, :]
    usable_slot = jnp.arange(capacity, dtype=jnp.int32)[None, :] < counts[:, None]
    clipped = jnp.minimum(source_rows, rows_dev - 1)
    send_rows = jnp.where(
        usable_slot[:, :, None], jnp.take(vectors, clipped, axis=0, mode="clip"), jnp.zeros((), jnp.bfloat16)
    )
    send_codes = jnp.take(codes, clipped, axis=0, mode="clip").astype(jnp.bfloat16)
    owner_base = (jnp.arange(owners, dtype=jnp.int32) * part_local)[:, None]
    send_ids = jnp.where(usable_slot, jnp.take(assign, clipped, axis=0, mode="clip") - owner_base, part_local)
    split_rows = send_rows.reshape(owners, capacity, sub_count, columns).transpose(0, 2, 1, 3)
    split_rows = split_rows.reshape(owners * sub_count, capacity, columns)
    split_codes = send_codes.reshape(owners, capacity, sub_count, local_sub).transpose(0, 2, 1, 3)
    split_codes = split_codes.reshape(owners * sub_count, capacity * local_sub // 128, 128)
    id_copies = jnp.broadcast_to(send_ids[:, None, :], (owners, sub_count, capacity))
    id_copies = id_copies.reshape(owners * sub_count, 1, capacity)
    slot_ids = lax.all_to_all(id_copies, ("dom", "sub"), split_axis=0, concat_axis=0, tiled=True)
    rows = lax.all_to_all(split_rows, ("dom", "sub"), split_axis=0, concat_axis=0, tiled=True)
    row_codes = lax.all_to_all(split_codes, ("dom", "sub"), split_axis=0, concat_axis=0, tiled=True)
    slot_ids = slot_ids.reshape(-1)
    rows = rows.reshape(-1, columns)
    row_codes = row_codes.reshape(-1, local_sub).astype(jnp.int32)
    usable = slot_ids < part_local
    safe_ids = jnp.minimum(slot_ids, part_local - 1)

    same = (slot_ids[:, None] == slot_ids[None, :]) & usable[:, None]
    same_table = same.astype(jnp.bfloat16)
    filled = jnp.sum(same.astype(jnp.float32), axis=1)
    floors = jnp.maximum(filled, 1.0)[:, None]
    sum_x = jnp.dot(same_table, rows, preferred_element_type=jnp.float32)
    as_float = rows.astype(jnp.float32)
    current = jnp.take(centroids, safe_ids, axis=0, mode="clip")
    digit_hi = slot_ids // ID_BASE
    digit_lo = slot_ids % ID_BASE
    block_count = part_local // ID_BASE
    pick_hi = (digit_hi[:, None] == jnp.arange(block_count, dtype=jnp.int32)[None, :]).astype(jnp.bfloat16)
    pick_lo = digit_lo[:, None] == jnp.arange(ID_BASE, dtype=jnp.int32)[None, :]
    weight_fractions = exact_pick(pick_hi, pick_lo, perp_ratio.reshape(block_count, ID_BASE))[:, None]
    filled_fraction = weight_fractions * filled[:, None]
    stats = shift_sum(
        jnp.stack([jnp.sum(as_float * as_float, axis=1), jnp.sum(as_float * current, axis=1)]), "sub"
    )
    norms = stats[0]
    inner = stats[1]
    for iteration in range(ITERS):
        if iteration > 0:
            inner = shift_sum(jnp.sum(as_float * current, axis=1), "sub")
        weight = inner / (norms + 1e-06)
        projected = split_dot(same_table, as_float * weight[:, None])
        current = (
            current
            - (filled_fraction * current + (1.0 - weight_fractions) * projected - sum_x) / floors
        )
    write_ids = jnp.where(usable, slot_ids, part_local)
    target = centroids + slot_ids[0].astype(jnp.float32) * 0.0
    new_centroids = target.at[write_ids].set(current, mode="drop")
    residual = jnp.where(usable[:, None], as_float - current, 0.0).astype(jnp.bfloat16)

    code_member = (
        (row_codes[:, :, None] == jnp.arange(code_count, dtype=jnp.int32)[None, None, :])
        & usable[:, None, None]
    ).astype(jnp.bfloat16)
    pieces = residual.reshape(-1, local_sub, sub_dim)
    book_sums = jnp.einsum("rmk,rmd->mkd", code_member, pieces, preferred_element_type=jnp.float32)
    book_counts = jnp.sum(code_member, axis=0, dtype=jnp.float32)
    packed = jnp.concatenate([book_sums.reshape(-1), book_counts.reshape(-1)])
    packed = butterfly_sum(packed.reshape(-1, 128), "dom").reshape(-1)
    entries = local_sub * code_count
    totals = packed[: entries * sub_dim].reshape(entries, sub_dim)
    tallies = packed[entries * sub_dim :]
    weights = codeword_weight_total.reshape(entries, 1)
    updated = (codebook.reshape(entries, sub_dim) * weights + totals) / (weights + tallies[:, None])

    outgoing = residual.reshape(owners * sub_count, capacity, columns)
    returned = lax.all_to_all(outgoing, ("dom", "sub"), split_axis=0, concat_axis=0, tiled=True)
    returned = returned.reshape(owners, sub_count, capacity, columns).transpose(0, 2, 1, 3)
    flat_rows = returned.reshape(owners * capacity, row_width)
    residual_rows = jnp.take(flat_rows, slot_index, axis=0, mode="clip")
    return (new_centroids, residual_rows, updated.reshape(local_sub, code_count, sub_dim))


def solution(mesh):
    placed = (
        P(("dom", "sub"), None),
        P(("dom", "sub")),
        P(("dom", "sub"), None),
        P("dom", "sub"),
        P("dom"),
        P("sub", None, None),
        P("sub", None),
    )
    return jax.shard_map(
        per_device,
        mesh=mesh,
        in_specs=placed,
        out_specs=(P("dom", "sub"), P(("dom", "sub"), None), P("sub", None, None)),
        check_vma=False,
    )
```

```python
import jax
import jax.numpy as jnp
from jax import lax
from jax.sharding import PartitionSpec as P

ITERS = 4
ID_BASE = 64


def split_dot(table, values):
    high = lax.reduce_precision(values, exponent_bits=8, mantissa_bits=7)
    low = (values - high).astype(jnp.bfloat16)
    width = values.shape[1]
    parts = jnp.concatenate([high.astype(jnp.bfloat16), low], axis=1)
    both = jnp.dot(table, parts, preferred_element_type=jnp.float32)
    return both[:, :width] + both[:, width:]


def exact_pick(pick_hi, pick_lo, table):
    high = lax.reduce_precision(table, exponent_bits=8, mantissa_bits=7)
    rest = table - high
    middle = lax.reduce_precision(rest, exponent_bits=8, mantissa_bits=7)
    low = rest - middle
    lanes = table.shape[1]
    parts = jnp.concatenate([high, middle, low], axis=1).astype(jnp.bfloat16)
    picked = jnp.dot(pick_hi, parts, preferred_element_type=jnp.float32)
    chosen = [
        jnp.sum(jnp.where(pick_lo, picked[:, k * lanes : (k + 1) * lanes], 0.0), axis=1) for k in range(3)
    ]
    return (chosen[0] + chosen[1]) + chosen[2]


def shift_sum(values, axis):
    count = lax.axis_size(axis)
    total = values
    for shift in range(1, count):
        pairs = [(source, (source + shift) % count) for source in range(count)]
        total = total + lax.ppermute(values, axis, pairs)
    return total


def butterfly_sum(values, axis):
    count = lax.axis_size(axis)
    total = values
    step = 1
    while step < count:
        pairs = [(source, source ^ step) for source in range(count)]
        total = total + lax.ppermute(total, axis, pairs)
        step *= 2
    return total


def per_device(vectors, assign, codes, centroids, perp_ratio, codebook, codeword_weight_total):
    owners = lax.axis_size("dom")
    sub_count = lax.axis_size("sub")
    rows_dev, row_width = vectors.shape
    part_local, columns = centroids.shape
    local_sub, code_count, sub_dim = codebook.shape
    capacity = 2 * rows_dev // owners

    owner_of = assign // part_local
    owner_mask = owner_of[:, None] == jnp.arange(owners, dtype=jnp.int32)[None, :]
    counts = jnp.sum(owner_mask.astype(jnp.int32), axis=0)
    starts = jnp.cumsum(counts) - counts
    first_row_index = jnp.sum(jnp.where(owner_mask, starts[None, :], 0), axis=1)
    position = jnp.arange(rows_dev, dtype=jnp.int32) - first_row_index
    slot_index = owner_of * capacity + position
    source_rows = starts[:, None] + jnp.arange(capacity, dtype=jnp.int32)[None, :]
    usable_slot = jnp.arange(capacity, dtype=jnp.int32)[None, :] < counts[:, None]
    clipped = jnp.minimum(source_rows, rows_dev - 1)
    send_rows = jnp.where(
        usable_slot[:, :, None], jnp.take(vectors, clipped, axis=0, mode="clip"), jnp.zeros((), jnp.bfloat16)
    )
    send_codes = jnp.take(codes, clipped, axis=0, mode="clip").astype(jnp.bfloat16)
    owner_base = (jnp.arange(owners, dtype=jnp.int32) * part_local)[:, None]
    send_ids = jnp.where(usable_slot, jnp.take(assign, clipped, axis=0, mode="clip") - owner_base, part_local)
    split_rows = send_rows.reshape(owners, capacity, sub_count, columns).transpose(0, 2, 1, 3)
    split_rows = split_rows.reshape(owners * sub_count, capacity, columns)
    split_codes = send_codes.reshape(owners, capacity, sub_count, local_sub).transpose(0, 2, 1, 3)
    split_codes = split_codes.reshape(owners * sub_count, capacity * local_sub // 128, 128)
    id_copies = jnp.broadcast_to(send_ids[:, None, :], (owners, sub_count, capacity))
    id_copies = id_copies.reshape(owners * sub_count, 1, capacity)
    slot_ids = lax.all_to_all(id_copies, ("dom", "sub"), split_axis=0, concat_axis=0, tiled=True)
    rows = lax.all_to_all(split_rows, ("dom", "sub"), split_axis=0, concat_axis=0, tiled=True)
    row_codes = lax.all_to_all(split_codes, ("dom", "sub"), split_axis=0, concat_axis=0, tiled=True)
    slot_ids = slot_ids.reshape(-1)
    rows = rows.reshape(-1, columns)
    row_codes = row_codes.reshape(-1, local_sub).astype(jnp.int32)
    usable = slot_ids < part_local
    safe_ids = jnp.minimum(slot_ids, part_local - 1)

    same = (slot_ids[:, None] == slot_ids[None, :]) & usable[:, None]
    same_table = same.astype(jnp.bfloat16)
    filled = jnp.sum(same.astype(jnp.float32), axis=1)
    floors = jnp.maximum(filled, 1.0)[:, None]
    sum_x = jnp.dot(same_table, rows, preferred_element_type=jnp.float32)
    as_float = rows.astype(jnp.float32)
    target = centroids + slot_ids[0].astype(jnp.float32) * 0.0
    current = jnp.take(target, safe_ids, axis=0, mode="clip")
    digit_hi = slot_ids // ID_BASE
    digit_lo = slot_ids % ID_BASE
    block_count = part_local // ID_BASE
    pick_hi = (digit_hi[:, None] == jnp.arange(block_count, dtype=jnp.int32)[None, :]).astype(jnp.bfloat16)
    pick_lo = digit_lo[:, None] == jnp.arange(ID_BASE, dtype=jnp.int32)[None, :]
    weight_fractions = exact_pick(pick_hi, pick_lo, perp_ratio.reshape(block_count, ID_BASE))[:, None]
    filled_fraction = weight_fractions * filled[:, None]
    stats = shift_sum(
        jnp.stack([jnp.sum(as_float * as_float, axis=1), jnp.sum(as_float * current, axis=1)]), "sub"
    )
    norms = stats[0]
    inner = stats[1]
    for iteration in range(ITERS):
        if iteration > 0:
            inner = shift_sum(jnp.sum(as_float * current, axis=1), "sub")
        weight = inner / (norms + 1e-06)
        projected = split_dot(same_table, as_float * weight[:, None])
        current = (
            current
            - (filled_fraction * current + (1.0 - weight_fractions) * projected - sum_x) / floors
        )
    write_ids = jnp.where(usable, slot_ids, part_local)
    new_centroids = target.at[write_ids].set(current, mode="drop")
    residual = jnp.where(usable[:, None], as_float - current, 0.0).astype(jnp.bfloat16)

    code_member = (
        (row_codes[:, :, None] == jnp.arange(code_count, dtype=jnp.int32)[None, None, :])
        & usable[:, None, None]
    ).astype(jnp.bfloat16)
    pieces = residual.reshape(-1, local_sub, sub_dim)
    book_sums = jnp.einsum("rmk,rmd->mkd", code_member, pieces, preferred_element_type=jnp.float32)
    book_counts = jnp.sum(code_member, axis=0, dtype=jnp.float32)
    packed = jnp.concatenate([book_sums.reshape(-1), book_counts.reshape(-1)])
    packed = butterfly_sum(packed.reshape(-1, 128), "dom").reshape(-1)
    entries = local_sub * code_count
    totals = packed[: entries * sub_dim].reshape(entries, sub_dim)
    tallies = packed[entries * sub_dim :]
    weights = codeword_weight_total.reshape(entries, 1)
    updated = (codebook.reshape(entries, sub_dim) * weights + totals) / (weights + tallies[:, None])

    outgoing = residual.reshape(owners * sub_count, capacity, columns)
    returned = lax.all_to_all(outgoing, ("dom", "sub"), split_axis=0, concat_axis=0, tiled=True)
    returned = returned.reshape(owners, sub_count, capacity, columns).transpose(0, 2, 1, 3)
    flat_rows = returned.reshape(owners * capacity, row_width)
    residual_rows = jnp.take(flat_rows, slot_index, axis=0, mode="clip")
    return (new_centroids, residual_rows, updated.reshape(local_sub, code_count, sub_dim))


def solution(mesh):
    placed = (
        P(("dom", "sub"), None),
        P(("dom", "sub")),
        P(("dom", "sub"), None),
        P("dom", "sub"),
        P("dom"),
        P("sub", None, None),
        P("sub", None),
    )
    return jax.shard_map(
        per_device,
        mesh=mesh,
        in_specs=placed,
        out_specs=(P("dom", "sub"), P(("dom", "sub"), None), P("sub", None, None)),
        check_vma=False,
    )
```

```python
import jax
import jax.numpy as jnp
from jax import lax
from jax.sharding import PartitionSpec as P

ITERS = 4
ID_BASE = 64


def split_dot(table, values):
    high = lax.reduce_precision(values, exponent_bits=8, mantissa_bits=7)
    low = (values - high).astype(jnp.bfloat16)
    width = values.shape[1]
    parts = jnp.concatenate([high.astype(jnp.bfloat16), low], axis=1)
    both = jnp.dot(table, parts, preferred_element_type=jnp.float32)
    return both[:, :width] + both[:, width:]


def exact_pick(pick_hi, pick_lo, table):
    high = lax.reduce_precision(table, exponent_bits=8, mantissa_bits=7)
    rest = table - high
    middle = lax.reduce_precision(rest, exponent_bits=8, mantissa_bits=7)
    low = rest - middle
    lanes = table.shape[1]
    parts = jnp.concatenate([high, middle, low], axis=1).astype(jnp.bfloat16)
    picked = jnp.dot(pick_hi, parts, preferred_element_type=jnp.float32)
    chosen = [
        jnp.sum(jnp.where(pick_lo, picked[:, k * lanes : (k + 1) * lanes], 0.0), axis=1) for k in range(3)
    ]
    return (chosen[0] + chosen[1]) + chosen[2]


def shift_sum(values, axis):
    count = lax.axis_size(axis)
    total = values
    for shift in range(1, count):
        pairs = [(source, (source + shift) % count) for source in range(count)]
        total = total + lax.ppermute(values, axis, pairs)
    return total


def butterfly_sum(values, axis):
    count = lax.axis_size(axis)
    total = values
    step = 1
    while step < count:
        pairs = [(source, source ^ step) for source in range(count)]
        total = total + lax.ppermute(total, axis, pairs)
        step *= 2
    return total


def per_device(vectors, assign, codes, centroids, perp_ratio, codebook, codeword_weight_total):
    owners = lax.axis_size("dom")
    sub_count = lax.axis_size("sub")
    rows_dev, row_width = vectors.shape
    part_local, columns = centroids.shape
    local_sub, code_count, sub_dim = codebook.shape
    capacity = 2 * rows_dev // owners

    owner_of = assign // part_local
    owner_mask = owner_of[:, None] == jnp.arange(owners, dtype=jnp.int32)[None, :]
    counts = jnp.sum(owner_mask.astype(jnp.int32), axis=0)
    starts = jnp.cumsum(counts) - counts
    first_row_index = jnp.sum(jnp.where(owner_mask, starts[None, :], 0), axis=1)
    position = jnp.arange(rows_dev, dtype=jnp.int32) - first_row_index
    source_rows = starts[:, None] + jnp.arange(capacity, dtype=jnp.int32)[None, :]
    usable_slot = jnp.arange(capacity, dtype=jnp.int32)[None, :] < counts[:, None]
    clipped = jnp.minimum(source_rows, rows_dev - 1)
    send_rows = jnp.where(
        usable_slot[:, :, None], jnp.take(vectors, clipped, axis=0, mode="clip"), jnp.zeros((), jnp.bfloat16)
    )
    send_codes = jnp.take(codes, clipped, axis=0, mode="clip").astype(jnp.bfloat16)
    owner_base = (jnp.arange(owners, dtype=jnp.int32) * part_local)[:, None]
    send_ids = jnp.where(usable_slot, jnp.take(assign, clipped, axis=0, mode="clip") - owner_base, part_local)
    split_rows = send_rows.reshape(owners, capacity, sub_count, columns).transpose(0, 2, 1, 3)
    split_rows = split_rows.reshape(owners * sub_count, capacity, columns)
    split_codes = send_codes.reshape(owners, capacity, sub_count, local_sub).transpose(0, 2, 1, 3)
    split_codes = split_codes.reshape(owners * sub_count, capacity * local_sub // 128, 128)
    id_copies = jnp.broadcast_to(send_ids[:, None, :], (owners, sub_count, capacity))
    id_copies = id_copies.reshape(owners * sub_count, 1, capacity)
    slot_ids = lax.all_to_all(id_copies, ("dom", "sub"), split_axis=0, concat_axis=0, tiled=True)
    rows = lax.all_to_all(split_rows, ("dom", "sub"), split_axis=0, concat_axis=0, tiled=True)
    row_codes = lax.all_to_all(split_codes, ("dom", "sub"), split_axis=0, concat_axis=0, tiled=True)
    slot_ids = slot_ids.reshape(-1)
    rows = rows.reshape(-1, columns)
    row_codes = row_codes.reshape(-1, local_sub).astype(jnp.int32)
    usable = slot_ids < part_local
    safe_ids = jnp.minimum(slot_ids, part_local - 1)

    same = (slot_ids[:, None] == slot_ids[None, :]) & usable[:, None]
    same_table = same.astype(jnp.bfloat16)
    filled = jnp.sum(same.astype(jnp.float32), axis=1)
    floors = jnp.maximum(filled, 1.0)[:, None]
    sum_x = jnp.dot(same_table, rows, preferred_element_type=jnp.float32)
    as_float = rows.astype(jnp.float32)
    target = centroids + slot_ids[0].astype(jnp.float32) * 0.0
    current = jnp.take(target, safe_ids, axis=0, mode="clip")
    digit_hi = slot_ids // ID_BASE
    digit_lo = slot_ids % ID_BASE
    block_count = part_local // ID_BASE
    pick_hi = (digit_hi[:, None] == jnp.arange(block_count, dtype=jnp.int32)[None, :]).astype(jnp.bfloat16)
    pick_lo = digit_lo[:, None] == jnp.arange(ID_BASE, dtype=jnp.int32)[None, :]
    weight_fractions = exact_pick(pick_hi, pick_lo, perp_ratio.reshape(block_count, ID_BASE))[:, None]
    filled_fraction = weight_fractions * filled[:, None]
    stats = shift_sum(
        jnp.stack([jnp.sum(as_float * as_float, axis=1), jnp.sum(as_float * current, axis=1)]), "sub"
    )
    norms = stats[0]
    inner = stats[1]
    for iteration in range(ITERS):
        if iteration > 0:
            inner = shift_sum(jnp.sum(as_float * current, axis=1), "sub")
        weight = inner / (norms + 1e-06)
        projected = split_dot(same_table, as_float * weight[:, None])
        current = (
            current
            - (filled_fraction * current + (1.0 - weight_fractions) * projected - sum_x) / floors
        )
    write_ids = jnp.where(usable, slot_ids, part_local)
    new_centroids = target.at[write_ids].set(current, mode="drop")
    residual = jnp.where(usable[:, None], as_float - current, 0.0).astype(jnp.bfloat16)

    code_member = (
        (row_codes[:, :, None] == jnp.arange(code_count, dtype=jnp.int32)[None, None, :])
        & usable[:, None, None]
    ).astype(jnp.bfloat16)
    pieces = residual.reshape(-1, local_sub, sub_dim)
    book_sums = jnp.einsum("rmk,rmd->mkd", code_member, pieces, preferred_element_type=jnp.float32)
    book_counts = jnp.sum(code_member, axis=0, dtype=jnp.float32)
    packed = jnp.concatenate([book_sums.reshape(-1), book_counts.reshape(-1)])
    packed = butterfly_sum(packed.reshape(-1, 128), "dom").reshape(-1)
    entries = local_sub * code_count
    totals = packed[: entries * sub_dim].reshape(entries, sub_dim)
    tallies = packed[entries * sub_dim :]
    weights = codeword_weight_total.reshape(entries, 1)
    updated = (codebook.reshape(entries, sub_dim) * weights + totals) / (weights + tallies[:, None])

    outgoing = residual.reshape(owners * sub_count, capacity, columns)
    returned = lax.all_to_all(outgoing, ("dom", "sub"), split_axis=0, concat_axis=0, tiled=True)
    block_of = owner_of[:, None] * sub_count + jnp.arange(sub_count, dtype=jnp.int32)[None, :]
    pick_rows = (block_of * capacity + position[:, None]).reshape(-1)
    residual_rows = jnp.take(returned.reshape(-1, columns), pick_rows, axis=0, mode="clip")
    residual_rows = residual_rows.reshape(rows_dev, row_width)
    return (new_centroids, residual_rows, updated.reshape(local_sub, code_count, sub_dim))


def solution(mesh):
    placed = (
        P(("dom", "sub"), None),
        P(("dom", "sub")),
        P(("dom", "sub"), None),
        P("dom", "sub"),
        P("dom"),
        P("sub", None, None),
        P("sub", None),
    )
    return jax.shard_map(
        per_device,
        mesh=mesh,
        in_specs=placed,
        out_specs=(P("dom", "sub"), P(("dom", "sub"), None), P("sub", None, None)),
        check_vma=False,
    )
```

```python
import jax
import jax.numpy as jnp
from jax import lax
from jax.sharding import PartitionSpec as P

ITERS = 4
ID_BASE = 64


def split_dot(table, values):
    high = lax.reduce_precision(values, exponent_bits=8, mantissa_bits=7)
    low = (values - high).astype(jnp.bfloat16)
    width = values.shape[1]
    parts = jnp.concatenate([high.astype(jnp.bfloat16), low], axis=1)
    both = jnp.dot(table, parts, preferred_element_type=jnp.float32)
    return both[:, :width] + both[:, width:]


def exact_pick(pick_hi, pick_lo, table):
    high = lax.reduce_precision(table, exponent_bits=8, mantissa_bits=7)
    rest = table - high
    middle = lax.reduce_precision(rest, exponent_bits=8, mantissa_bits=7)
    low = rest - middle
    lanes = table.shape[1]
    parts = jnp.concatenate([high, middle, low], axis=1).astype(jnp.bfloat16)
    picked = jnp.dot(pick_hi, parts, preferred_element_type=jnp.float32)
    chosen = [
        jnp.sum(jnp.where(pick_lo, picked[:, k * lanes : (k + 1) * lanes], 0.0), axis=1) for k in range(3)
    ]
    return (chosen[0] + chosen[1]) + chosen[2]


def shift_sum(values, axis):
    count = lax.axis_size(axis)
    total = values
    for shift in range(1, count):
        pairs = [(source, (source + shift) % count) for source in range(count)]
        total = total + lax.ppermute(values, axis, pairs)
    return total


def butterfly_sum(values, axis):
    count = lax.axis_size(axis)
    total = values
    step = 1
    while step < count:
        pairs = [(source, source ^ step) for source in range(count)]
        total = total + lax.ppermute(total, axis, pairs)
        step *= 2
    return total


def per_device(vectors, assign, codes, centroids, perp_ratio, codebook, codeword_weight_total):
    owners = lax.axis_size("dom")
    sub_count = lax.axis_size("sub")
    rows_dev, row_width = vectors.shape
    part_local, columns = centroids.shape
    local_sub, code_count, sub_dim = codebook.shape
    capacity = 2 * rows_dev // owners

    owner_of = assign // part_local
    owner_mask = owner_of[:, None] == jnp.arange(owners, dtype=jnp.int32)[None, :]
    counts = jnp.sum(owner_mask.astype(jnp.int32), axis=0)
    starts = jnp.cumsum(counts) - counts
    first_row_index = jnp.sum(jnp.where(owner_mask, starts[None, :], 0), axis=1)
    position = jnp.arange(rows_dev, dtype=jnp.int32) - first_row_index
    slot_index = owner_of * capacity + position
    source_rows = starts[:, None] + jnp.arange(capacity, dtype=jnp.int32)[None, :]
    usable_slot = jnp.arange(capacity, dtype=jnp.int32)[None, :] < counts[:, None]
    clipped = jnp.minimum(source_rows, rows_dev - 1)
    send_rows = jnp.where(
        usable_slot[:, :, None], jnp.take(vectors, clipped, axis=0, mode="clip"), jnp.zeros((), jnp.bfloat16)
    )
    owner_base = (jnp.arange(owners, dtype=jnp.int32) * part_local)[:, None]
    send_ids = jnp.where(usable_slot, jnp.take(assign, clipped, axis=0, mode="clip") - owner_base, part_local)
    split_rows = send_rows.reshape(owners, capacity, sub_count, columns).transpose(0, 2, 1, 3)
    split_rows = split_rows.reshape(owners * sub_count, capacity, columns)
    id_copies = jnp.broadcast_to(send_ids[:, None, :], (owners, sub_count, capacity))
    id_copies = id_copies.reshape(owners * sub_count, 1, capacity)
    slot_ids = lax.all_to_all(id_copies, ("dom", "sub"), split_axis=0, concat_axis=0, tiled=True)
    rows = lax.all_to_all(split_rows, ("dom", "sub"), split_axis=0, concat_axis=0, tiled=True)
    late_rows = jnp.minimum(clipped, jnp.maximum(slot_ids[0, 0, 0], rows_dev - 1))
    send_codes = jnp.take(codes, late_rows, axis=0, mode="clip").astype(jnp.bfloat16)
    split_codes = send_codes.reshape(owners, capacity, sub_count, local_sub).transpose(0, 2, 1, 3)
    split_codes = split_codes.reshape(owners * sub_count, capacity * local_sub // 128, 128)
    row_codes = lax.all_to_all(split_codes, ("dom", "sub"), split_axis=0, concat_axis=0, tiled=True)
    slot_ids = slot_ids.reshape(-1)
    rows = rows.reshape(-1, columns)
    row_codes = row_codes.reshape(-1, local_sub).astype(jnp.int32)
    usable = slot_ids < part_local
    safe_ids = jnp.minimum(slot_ids, part_local - 1)

    same = (slot_ids[:, None] == slot_ids[None, :]) & usable[:, None]
    same_table = same.astype(jnp.bfloat16)
    filled = jnp.sum(same.astype(jnp.float32), axis=1)
    floors = jnp.maximum(filled, 1.0)[:, None]
    sum_x = jnp.dot(same_table, rows, preferred_element_type=jnp.float32)
    as_float = rows.astype(jnp.float32)
    target = centroids + slot_ids[0].astype(jnp.float32) * 0.0
    current = jnp.take(target, safe_ids, axis=0, mode="clip")
    digit_hi = slot_ids // ID_BASE
    digit_lo = slot_ids % ID_BASE
    block_count = part_local // ID_BASE
    pick_hi = (digit_hi[:, None] == jnp.arange(block_count, dtype=jnp.int32)[None, :]).astype(jnp.bfloat16)
    pick_lo = digit_lo[:, None] == jnp.arange(ID_BASE, dtype=jnp.int32)[None, :]
    weight_fractions = exact_pick(pick_hi, pick_lo, perp_ratio.reshape(block_count, ID_BASE))[:, None]
    filled_fraction = weight_fractions * filled[:, None]
    stats = shift_sum(
        jnp.stack([jnp.sum(as_float * as_float, axis=1), jnp.sum(as_float * current, axis=1)]), "sub"
    )
    norms = stats[0]
    inner = stats[1]
    for iteration in range(ITERS):
        if iteration > 0:
            inner = shift_sum(jnp.sum(as_float * current, axis=1), "sub")
        weight = inner / (norms + 1e-06)
        projected = split_dot(same_table, as_float * weight[:, None])
        current = (
            current
            - (filled_fraction * current + (1.0 - weight_fractions) * projected - sum_x) / floors
        )
    write_ids = jnp.where(usable, slot_ids, part_local)
    new_centroids = target.at[write_ids].set(current, mode="drop")
    residual = jnp.where(usable[:, None], as_float - current, 0.0).astype(jnp.bfloat16)

    code_member = (
        (row_codes[:, :, None] == jnp.arange(code_count, dtype=jnp.int32)[None, None, :])
        & usable[:, None, None]
    ).astype(jnp.bfloat16)
    pieces = residual.reshape(-1, local_sub, sub_dim)
    book_sums = jnp.einsum("rmk,rmd->mkd", code_member, pieces, preferred_element_type=jnp.float32)
    book_counts = jnp.sum(code_member, axis=0, dtype=jnp.float32)
    packed = jnp.concatenate([book_sums.reshape(-1), book_counts.reshape(-1)])
    packed = butterfly_sum(packed.reshape(-1, 128), "dom").reshape(-1)
    entries = local_sub * code_count
    totals = packed[: entries * sub_dim].reshape(entries, sub_dim)
    tallies = packed[entries * sub_dim :]
    weights = codeword_weight_total.reshape(entries, 1)
    updated = (codebook.reshape(entries, sub_dim) * weights + totals) / (weights + tallies[:, None])

    outgoing = residual.reshape(owners * sub_count, capacity, columns)
    returned = lax.all_to_all(outgoing, ("dom", "sub"), split_axis=0, concat_axis=0, tiled=True)
    returned = returned.reshape(owners, sub_count, capacity, columns).transpose(0, 2, 1, 3)
    flat_rows = returned.reshape(owners * capacity, row_width)
    residual_rows = jnp.take(flat_rows, slot_index, axis=0, mode="clip")
    return (new_centroids, residual_rows, updated.reshape(local_sub, code_count, sub_dim))


def solution(mesh):
    placed = (
        P(("dom", "sub"), None),
        P(("dom", "sub")),
        P(("dom", "sub"), None),
        P("dom", "sub"),
        P("dom"),
        P("sub", None, None),
        P("sub", None),
    )
    return jax.shard_map(
        per_device,
        mesh=mesh,
        in_specs=placed,
        out_specs=(P("dom", "sub"), P(("dom", "sub"), None), P("sub", None, None)),
        check_vma=False,
    )
```

```python
import jax
import jax.numpy as jnp
from jax import lax
from jax.sharding import PartitionSpec as P

ITERS = 4
ID_BASE = 64


def split_dot(doubled_table, values):
    high = lax.reduce_precision(values, exponent_bits=8, mantissa_bits=7)
    low = (values - high).astype(jnp.bfloat16)
    parts = jnp.concatenate([high.astype(jnp.bfloat16), low], axis=0)
    return jnp.dot(doubled_table, parts, preferred_element_type=jnp.float32)


def exact_pick(pick_hi, pick_lo, table):
    high = lax.reduce_precision(table, exponent_bits=8, mantissa_bits=7)
    rest = table - high
    middle = lax.reduce_precision(rest, exponent_bits=8, mantissa_bits=7)
    low = rest - middle
    lanes = table.shape[1]
    parts = jnp.concatenate([high, middle, low], axis=1).astype(jnp.bfloat16)
    picked = jnp.dot(pick_hi, parts, preferred_element_type=jnp.float32)
    chosen = [
        jnp.sum(jnp.where(pick_lo, picked[:, k * lanes : (k + 1) * lanes], 0.0), axis=1) for k in range(3)
    ]
    return (chosen[0] + chosen[1]) + chosen[2]


def shift_sum(values, axis):
    count = lax.axis_size(axis)
    total = values
    for shift in range(1, count):
        pairs = [(source, (source + shift) % count) for source in range(count)]
        total = total + lax.ppermute(values, axis, pairs)
    return total


def butterfly_sum(values, axis):
    count = lax.axis_size(axis)
    total = values
    step = 1
    while step < count:
        pairs = [(source, source ^ step) for source in range(count)]
        total = total + lax.ppermute(total, axis, pairs)
        step *= 2
    return total


def per_device(vectors, assign, codes, centroids, perp_ratio, codebook, codeword_weight_total):
    owners = lax.axis_size("dom")
    sub_count = lax.axis_size("sub")
    rows_dev, row_width = vectors.shape
    part_local, columns = centroids.shape
    local_sub, code_count, sub_dim = codebook.shape
    capacity = 2 * rows_dev // owners

    owner_of = assign // part_local
    owner_mask = owner_of[:, None] == jnp.arange(owners, dtype=jnp.int32)[None, :]
    counts = jnp.sum(owner_mask.astype(jnp.int32), axis=0)
    starts = jnp.cumsum(counts) - counts
    first_row_index = jnp.sum(jnp.where(owner_mask, starts[None, :], 0), axis=1)
    position = jnp.arange(rows_dev, dtype=jnp.int32) - first_row_index
    slot_index = owner_of * capacity + position
    source_rows = starts[:, None] + jnp.arange(capacity, dtype=jnp.int32)[None, :]
    usable_slot = jnp.arange(capacity, dtype=jnp.int32)[None, :] < counts[:, None]
    clipped = jnp.minimum(source_rows, rows_dev - 1)
    send_rows = jnp.where(
        usable_slot[:, :, None], jnp.take(vectors, clipped, axis=0, mode="clip"), jnp.zeros((), jnp.bfloat16)
    )
    send_codes = jnp.take(codes, clipped, axis=0, mode="clip").astype(jnp.bfloat16)
    owner_base = (jnp.arange(owners, dtype=jnp.int32) * part_local)[:, None]
    send_ids = jnp.where(usable_slot, jnp.take(assign, clipped, axis=0, mode="clip") - owner_base, part_local)
    split_rows = send_rows.reshape(owners, capacity, sub_count, columns).transpose(0, 2, 1, 3)
    split_rows = split_rows.reshape(owners * sub_count, capacity, columns)
    split_codes = send_codes.reshape(owners, capacity, sub_count, local_sub).transpose(0, 2, 1, 3)
    split_codes = split_codes.reshape(owners * sub_count, capacity * local_sub // 128, 128)
    id_copies = jnp.broadcast_to(send_ids[:, None, :], (owners, sub_count, capacity))
    id_copies = id_copies.reshape(owners * sub_count, 1, capacity)
    slot_ids = lax.all_to_all(id_copies, ("dom", "sub"), split_axis=0, concat_axis=0, tiled=True)
    rows = lax.all_to_all(split_rows, ("dom", "sub"), split_axis=0, concat_axis=0, tiled=True)
    row_codes = lax.all_to_all(split_codes, ("dom", "sub"), split_axis=0, concat_axis=0, tiled=True)
    slot_ids = slot_ids.reshape(-1)
    rows = rows.reshape(-1, columns)
    row_codes = row_codes.reshape(-1, local_sub).astype(jnp.int32)
    usable = slot_ids < part_local
    safe_ids = jnp.minimum(slot_ids, part_local - 1)

    same = (slot_ids[:, None] == slot_ids[None, :]) & usable[:, None]
    same_table = same.astype(jnp.bfloat16)
    doubled_table = jnp.concatenate([same_table, same_table], axis=1)
    filled = jnp.sum(same.astype(jnp.float32), axis=1)
    floors = jnp.maximum(filled, 1.0)[:, None]
    sum_x = jnp.dot(same_table, rows, preferred_element_type=jnp.float32)
    as_float = rows.astype(jnp.float32)
    target = centroids + slot_ids[0].astype(jnp.float32) * 0.0
    current = jnp.take(target, safe_ids, axis=0, mode="clip")
    digit_hi = slot_ids // ID_BASE
    digit_lo = slot_ids % ID_BASE
    block_count = part_local // ID_BASE
    pick_hi = (digit_hi[:, None] == jnp.arange(block_count, dtype=jnp.int32)[None, :]).astype(jnp.bfloat16)
    pick_lo = digit_lo[:, None] == jnp.arange(ID_BASE, dtype=jnp.int32)[None, :]
    weight_fractions = exact_pick(pick_hi, pick_lo, perp_ratio.reshape(block_count, ID_BASE))[:, None]
    filled_fraction = weight_fractions * filled[:, None]
    stats = shift_sum(
        jnp.stack([jnp.sum(as_float * as_float, axis=1), jnp.sum(as_float * current, axis=1)]), "sub"
    )
    norms = stats[0]
    inner = stats[1]
    for iteration in range(ITERS):
        if iteration > 0:
            inner = shift_sum(jnp.sum(as_float * current, axis=1), "sub")
        weight = inner / (norms + 1e-06)
        projected = split_dot(doubled_table, as_float * weight[:, None])
        current = (
            current
            - (filled_fraction * current + (1.0 - weight_fractions) * projected - sum_x) / floors
        )
    write_ids = jnp.where(usable, slot_ids, part_local)
    new_centroids = target.at[write_ids].set(current, mode="drop")
    residual = jnp.where(usable[:, None], as_float - current, 0.0).astype(jnp.bfloat16)

    code_member = (
        (row_codes[:, :, None] == jnp.arange(code_count, dtype=jnp.int32)[None, None, :])
        & usable[:, None, None]
    ).astype(jnp.bfloat16)
    pieces = residual.reshape(-1, local_sub, sub_dim)
    book_sums = jnp.einsum("rmk,rmd->mkd", code_member, pieces, preferred_element_type=jnp.float32)
    book_counts = jnp.sum(code_member, axis=0, dtype=jnp.float32)
    packed = jnp.concatenate([book_sums.reshape(-1), book_counts.reshape(-1)])
    packed = butterfly_sum(packed.reshape(-1, 128), "dom").reshape(-1)
    entries = local_sub * code_count
    totals = packed[: entries * sub_dim].reshape(entries, sub_dim)
    tallies = packed[entries * sub_dim :]
    weights = codeword_weight_total.reshape(entries, 1)
    updated = (codebook.reshape(entries, sub_dim) * weights + totals) / (weights + tallies[:, None])

    outgoing = residual.reshape(owners * sub_count, capacity, columns)
    returned = lax.all_to_all(outgoing, ("dom", "sub"), split_axis=0, concat_axis=0, tiled=True)
    returned = returned.reshape(owners, sub_count, capacity, columns).transpose(0, 2, 1, 3)
    flat_rows = returned.reshape(owners * capacity, row_width)
    residual_rows = jnp.take(flat_rows, slot_index, axis=0, mode="clip")
    return (new_centroids, residual_rows, updated.reshape(local_sub, code_count, sub_dim))


def solution(mesh):
    placed = (
        P(("dom", "sub"), None),
        P(("dom", "sub")),
        P(("dom", "sub"), None),
        P("dom", "sub"),
        P("dom"),
        P("sub", None, None),
        P("sub", None),
    )
    return jax.shard_map(
        per_device,
        mesh=mesh,
        in_specs=placed,
        out_specs=(P("dom", "sub"), P(("dom", "sub"), None), P("sub", None, None)),
        check_vma=False,
    )
```

```python
import jax
import jax.numpy as jnp
from jax import lax
from jax.sharding import PartitionSpec as P

ITERS = 4
ID_BASE = 64


def split_dot(table, values):
    high = lax.reduce_precision(values, exponent_bits=8, mantissa_bits=7)
    low = (values - high).astype(jnp.bfloat16)
    width = values.shape[1]
    parts = jnp.concatenate([high.astype(jnp.bfloat16), low], axis=1)
    both = jnp.dot(table, parts, preferred_element_type=jnp.float32)
    return both[:, :width] + both[:, width:]


def exact_pick(pick_hi, pick_lo, table):
    high = lax.reduce_precision(table, exponent_bits=8, mantissa_bits=7)
    rest = table - high
    middle = lax.reduce_precision(rest, exponent_bits=8, mantissa_bits=7)
    low = rest - middle
    lanes = table.shape[1]
    parts = jnp.concatenate([high, middle, low], axis=1).astype(jnp.bfloat16)
    picked = jnp.dot(pick_hi, parts, preferred_element_type=jnp.float32)
    chosen = [
        jnp.sum(jnp.where(pick_lo, picked[:, k * lanes : (k + 1) * lanes], 0.0), axis=1) for k in range(3)
    ]
    return (chosen[0] + chosen[1]) + chosen[2]


def shift_sum(values, axis):
    count = lax.axis_size(axis)
    total = values
    for shift in range(1, count):
        pairs = [(source, (source + shift) % count) for source in range(count)]
        total = total + lax.ppermute(values, axis, pairs)
    return total


def butterfly_sum(values, axis):
    count = lax.axis_size(axis)
    total = values
    step = 1
    while step < count:
        pairs = [(source, source ^ step) for source in range(count)]
        total = total + lax.ppermute(total, axis, pairs)
        step *= 2
    return total


def per_device(vectors, assign, codes, centroids, perp_ratio, codebook, codeword_weight_total):
    owners = lax.axis_size("dom")
    sub_count = lax.axis_size("sub")
    rows_dev, row_width = vectors.shape
    part_local, columns = centroids.shape
    local_sub, code_count, sub_dim = codebook.shape
    capacity = 2 * rows_dev // owners

    owner_of = assign // part_local
    owner_mask = owner_of[:, None] == jnp.arange(owners, dtype=jnp.int32)[None, :]
    counts = jnp.sum(owner_mask.astype(jnp.int32), axis=0)
    starts = jnp.cumsum(counts) - counts
    first_row_index = jnp.sum(jnp.where(owner_mask, starts[None, :], 0), axis=1)
    position = jnp.arange(rows_dev, dtype=jnp.int32) - first_row_index
    slot_index = owner_of * capacity + position
    source_rows = starts[:, None] + jnp.arange(capacity, dtype=jnp.int32)[None, :]
    usable_slot = jnp.arange(capacity, dtype=jnp.int32)[None, :] < counts[:, None]
    clipped = jnp.minimum(source_rows, rows_dev - 1)
    send_rows = jnp.where(
        usable_slot[:, :, None], jnp.take(vectors, clipped, axis=0, mode="clip"), jnp.zeros((), jnp.bfloat16)
    )
    send_codes = jnp.take(codes, clipped, axis=0, mode="clip").astype(jnp.bfloat16)
    owner_base = (jnp.arange(owners, dtype=jnp.int32) * part_local)[:, None]
    send_ids = jnp.where(usable_slot, jnp.take(assign, clipped, axis=0, mode="clip") - owner_base, part_local)
    split_rows = send_rows.reshape(owners, capacity, sub_count, columns).transpose(0, 2, 1, 3)
    split_rows = split_rows.reshape(owners * sub_count, capacity, columns)
    split_codes = send_codes.reshape(owners, capacity, sub_count, local_sub).transpose(0, 2, 1, 3)
    split_codes = split_codes.reshape(owners * sub_count, capacity * local_sub // 128, 128)
    id_copies = jnp.broadcast_to(send_ids[:, None, :], (owners, sub_count, capacity))
    id_copies = id_copies.reshape(owners * sub_count, 1, capacity)
    slot_ids = lax.all_to_all(id_copies, ("dom", "sub"), split_axis=0, concat_axis=0, tiled=True)
    rows = lax.all_to_all(split_rows, ("dom", "sub"), split_axis=0, concat_axis=0, tiled=True)
    row_codes = lax.all_to_all(split_codes, ("dom", "sub"), split_axis=0, concat_axis=0, tiled=True)
    slot_ids = slot_ids.reshape(-1)
    rows = rows.reshape(-1, columns)
    row_codes = row_codes.reshape(-1, local_sub).astype(jnp.int32)
    usable = slot_ids < part_local
    safe_ids = jnp.minimum(slot_ids, part_local - 1)

    same = (slot_ids[:, None] == slot_ids[None, :]) & usable[:, None]
    same_table = same.astype(jnp.bfloat16)
    filled = jnp.sum(same.astype(jnp.float32), axis=1)
    inverse_floors = 1.0 / jnp.maximum(filled, 1.0)[:, None]
    sum_x = jnp.dot(same_table, rows, preferred_element_type=jnp.float32)
    as_float = rows.astype(jnp.float32)
    target = centroids + slot_ids[0].astype(jnp.float32) * 0.0
    current = jnp.take(target, safe_ids, axis=0, mode="clip")
    digit_hi = slot_ids // ID_BASE
    digit_lo = slot_ids % ID_BASE
    block_count = part_local // ID_BASE
    pick_hi = (digit_hi[:, None] == jnp.arange(block_count, dtype=jnp.int32)[None, :]).astype(jnp.bfloat16)
    pick_lo = digit_lo[:, None] == jnp.arange(ID_BASE, dtype=jnp.int32)[None, :]
    weight_fractions = exact_pick(pick_hi, pick_lo, perp_ratio.reshape(block_count, ID_BASE))[:, None]
    filled_fraction = weight_fractions * filled[:, None]
    stats = shift_sum(
        jnp.stack([jnp.sum(as_float * as_float, axis=1), jnp.sum(as_float * current, axis=1)]), "sub"
    )
    norms = stats[0]
    inner = stats[1]
    for iteration in range(ITERS):
        if iteration > 0:
            inner = shift_sum(jnp.sum(as_float * current, axis=1), "sub")
        weight = inner / (norms + 1e-06)
        projected = split_dot(same_table, as_float * weight[:, None])
        current = (
            current
            - (filled_fraction * current + (1.0 - weight_fractions) * projected - sum_x) * inverse_floors
        )
    write_ids = jnp.where(usable, slot_ids, part_local)
    new_centroids = target.at[write_ids].set(current, mode="drop")
    residual = jnp.where(usable[:, None], as_float - current, 0.0).astype(jnp.bfloat16)

    code_member = (
        (row_codes[:, :, None] == jnp.arange(code_count, dtype=jnp.int32)[None, None, :])
        & usable[:, None, None]
    ).astype(jnp.bfloat16)
    pieces = residual.reshape(-1, local_sub, sub_dim)
    book_sums = jnp.einsum("rmk,rmd->mkd", code_member, pieces, preferred_element_type=jnp.float32)
    book_counts = jnp.sum(code_member, axis=0, dtype=jnp.float32)
    packed = jnp.concatenate([book_sums.reshape(-1), book_counts.reshape(-1)])
    packed = butterfly_sum(packed.reshape(-1, 128), "dom").reshape(-1)
    entries = local_sub * code_count
    totals = packed[: entries * sub_dim].reshape(entries, sub_dim)
    tallies = packed[entries * sub_dim :]
    weights = codeword_weight_total.reshape(entries, 1)
    updated = (codebook.reshape(entries, sub_dim) * weights + totals) / (weights + tallies[:, None])

    outgoing = residual.reshape(owners * sub_count, capacity, columns)
    returned = lax.all_to_all(outgoing, ("dom", "sub"), split_axis=0, concat_axis=0, tiled=True)
    returned = returned.reshape(owners, sub_count, capacity, columns).transpose(0, 2, 1, 3)
    flat_rows = returned.reshape(owners * capacity, row_width)
    residual_rows = jnp.take(flat_rows, slot_index, axis=0, mode="clip")
    return (new_centroids, residual_rows, updated.reshape(local_sub, code_count, sub_dim))


def solution(mesh):
    placed = (
        P(("dom", "sub"), None),
        P(("dom", "sub")),
        P(("dom", "sub"), None),
        P("dom", "sub"),
        P("dom"),
        P("sub", None, None),
        P("sub", None),
    )
    return jax.shard_map(
        per_device,
        mesh=mesh,
        in_specs=placed,
        out_specs=(P("dom", "sub"), P(("dom", "sub"), None), P("sub", None, None)),
        check_vma=False,
    )
```
